32 devices in a mesh: groups: 2 (over y), scan: 4 (over z), depth: 4 (over x, core).
Axes of the slice: x: 2, y: 2, z: 4, core: 2. Of those that a mesh axis runs over, the one named last changes fastest.
Arguments:
- probe: float32 [2, 256, 256], replicated, may hold values from -6 to 6
- slices: float32 [8, 2, 2048, 1024], P('depth', None, ('groups', 'scan')), parts along dimension 2, may hold values from -3 to 3, as said below
- positions: int32 [16, 2], P(('groups', 'scan')), parts along dimension 0, may hold values from 0 to 768, as said below
- counts: int32 [8], P(('groups', 'scan')), parts along dimension 0, may hold values from 1 to 2, as said below
- amplitude: float32 [16, 256, 256], P(('groups', 'scan')), parts along dimension 0, may hold values from 0.2 to 3
Outputs:
- gradient: float32 [8, 2, 2048, 1024], P('depth', None, ('groups', 'scan')), parts along dimension 2
The draws below stay inside these ranges and needn't reach their ends.
There are 2 independent parts, one for each index of `groups`. The reference program is written for one: setup_inputs(seed, part) draws one part's arguments, and reference() takes and returns one part's arrays. A program takes and returns all parts, laid end to end along the dimension named above; an argument that names none is the same for every part. Nothing has to cross between parts.
Inputs may be any that keep to these rules, and one draw needn't show every extreme that they name: `positions`: row offsets lie in 0 to 255 and column offsets in 0 to 768; both ends of both ranges are taken. `counts`: each tile has 1 to 2 live patches, in its first slots; some tile has 2 and some has 1. `slices`: transmission of magnitude between exp(-1) and exp(1).
All inputs are finite; a program needn't handle non-finite values.
Results may differ from the reference program's by a relative error of at most 0.0003.
Values sent between devices are 32-bit elements; how exact they have to be, the bound alone decides.
No kernel may reach another device: no remote copies, remote signals or barrier semaphores. Data moves between devices by JAX's collectives and lax.ppermute only.
A program may use at most 128 MiB of HBM per device.

```python
import math
import jax
import jax.numpy as jnp
from jax import lax

PATCH = 256
WIDTH = 1024
SLOTS = 2
SLICES = 8
TILES = 4
ROWS = 1024


def draw_slices(key, part):
    key_level = jax.random.fold_in(key, 11)
    key_phase = jax.random.fold_in(key, 12)
    shape = (SLICES, ROWS, WIDTH)
    level = jnp.clip(0.25 * jax.random.normal(key_level, shape, jnp.float32), -1.0, 1.0)
    phase = jnp.clip(0.6 * jax.random.normal(key_phase, shape, jnp.float32), -2.4, 2.4)
    magnitude = jnp.exp(level)
    return jnp.stack([magnitude * jnp.cos(phase), magnitude * jnp.sin(phase)], axis=1)


def draw_positions(key, part):
    total = ROWS // PATCH * SLOTS
    row_offsets = jax.random.randint(jax.random.fold_in(key, 21), (total,), 0, PATCH)
    col_offsets = jax.random.randint(jax.random.fold_in(key, 22), (total,), 0, WIDTH - PATCH + 1)
    first = jax.random.randint(jax.random.fold_in(key, 23), (), 0, total)
    second = (first + 1) % total
    row_offsets = row_offsets.at[first].set(PATCH - 1).at[second].set(0)
    col_offsets = col_offsets.at[first].set(WIDTH - PATCH).at[second].set(0)
    return jnp.stack([row_offsets, col_offsets], axis=1).astype(jnp.int32)


def draw_counts(key, part):
    tiles = ROWS // PATCH
    values = jax.random.randint(jax.random.fold_in(key, 31), (tiles,), 1, SLOTS + 1)
    first = jax.random.randint(jax.random.fold_in(key, 32), (), 0, tiles)
    second = (first + 1) % tiles
    return values.at[first].set(SLOTS).at[second].set(1).astype(jnp.int32)


def block_scale(stream_key, extent, shards, low, largest):
    level = 1.0
    for position, shards_of in shards:
        heights = jax.random.uniform(jax.random.fold_in(jax.random.fold_in(stream_key, 6), position), (shards_of,), jnp.float32, low / len(shards), largest / len(shards))
        level = level * jnp.repeat(jnp.exp(heights), extent[position] // shards_of).reshape((-1,) + (1,) * (len(extent) - 1 - position))
    return level


def gaussian(key, shape, width, limit, kind=jnp.bfloat16):
    drawn = jax.random.normal(key, shape, jnp.float32) * width
    return jnp.minimum(jnp.maximum(drawn, -limit), limit).astype(kind)


def setup_inputs(seed: int = 0, part: int = 0) -> dict:
    splits = jax.random.split(jax.random.key(seed), 6)
    own_keys = jax.random.split(jax.random.fold_in(splits[5], part), 6)
    probe = gaussian(splits[0], (2, PATCH, PATCH), 1.0, 6.0, jnp.float32)
    slices = draw_slices(jax.random.fold_in(jax.random.fold_in(splits[5], part), 71), part)
    positions = draw_positions(jax.random.fold_in(jax.random.fold_in(splits[5], part), 71), part)
    counts = draw_counts(jax.random.fold_in(jax.random.fold_in(splits[5], part), 71), part)
    amplitude = jnp.clip(jnp.exp(math.log(3.0) - 2.7080502 * jax.random.uniform(own_keys[4], (TILES * SLOTS, PATCH, PATCH), jnp.float32) ** block_scale(own_keys[4], (TILES * SLOTS, PATCH, PATCH), ((0, 4),), -0.2, 0.2)), 0.2, 3.0)
    return {"probe": probe, "slices": slices, "positions": positions, "counts": counts, "amplitude": amplitude}


chirp_rate = 0.25

def make_tables(length):
    index = jnp.arange(length, dtype=jnp.int32)
    product = index[:, None] * index[None, :] % length
    angle = 2.0 * math.pi / length * product.astype(jnp.float32)
    factor = 1.0 / math.sqrt(length)
    table_real = (jnp.cos(angle) * factor).astype(jnp.float32)
    table_imag = (-jnp.sin(angle) * factor).astype(jnp.float32)
    freq = jnp.where(index < length // 2, index, index - length).astype(jnp.float32)
    theta = -math.pi * chirp_rate / length * (freq[:, None] ** 2 + freq[None, :] ** 2)
    return (table_real, table_imag, jnp.cos(theta), jnp.sin(theta))

def left_product(matrix, field):
    return jnp.einsum('jk,...kl->...jl', matrix.astype(jnp.float32), field.astype(jnp.float32), precision=lax.Precision.HIGHEST)

def right_product(field, matrix):
    return jnp.einsum('...jk,kl->...jl', field.astype(jnp.float32), matrix.astype(jnp.float32), precision=lax.Precision.HIGHEST)

def transform(field, tables, forward):
    table_real = tables[0]
    table_imag = tables[1] if forward else -tables[1]
    real_part = field[..., 0, :, :]
    imag_part = field[..., 1, :, :]
    first_real = left_product(table_real, real_part) - left_product(table_imag, imag_part)
    first_imag = left_product(table_real, imag_part) + left_product(table_imag, real_part)
    out_real = right_product(first_real, table_real) - right_product(first_imag, table_imag)
    out_imag = right_product(first_real, table_imag) + right_product(first_imag, table_real)
    return jnp.stack([out_real, out_imag], axis=-3)

def complex_product(first, second, conjugate):
    first_real = first[..., 0, :, :].astype(jnp.float32)
    first_imag = first[..., 1, :, :].astype(jnp.float32)
    if conjugate:
        first_imag = -first_imag
    second_real = second[..., 0, :, :].astype(jnp.float32)
    second_imag = second[..., 1, :, :].astype(jnp.float32)
    return jnp.stack([first_real * second_real - first_imag * second_imag, first_real * second_imag + first_imag * second_real], axis=-3)

def propagate(field, tables, forward):
    spectrum = transform(field, tables, True)
    sine = tables[3] if forward else -tables[3]
    chirp = jnp.stack([tables[2], sine], axis=0)
    return transform(complex_product(spectrum, chirp, False), tables, False)

def far_field(exit_wave, measured, live, tables):
    spectrum = transform(exit_wave, tables, True)
    power = spectrum[..., 0, :, :] ** 2 + spectrum[..., 1, :, :] ** 2
    keep = live * (1.0 - measured.astype(jnp.float32) / jnp.sqrt(power + 1.0))
    residual = spectrum * keep[..., None, :, :]
    return transform(residual, tables, False)

def reference(probe, slices, positions, counts, amplitude):
    tables = make_tables(PATCH)
    tiles = ROWS // PATCH
    places = positions.astype(jnp.int32)
    live_counts = counts.astype(jnp.int32)
    extended = jnp.concatenate([slices, slices[:, :, :PATCH]], axis=2).astype(jnp.float32)
    start_wave = probe.astype(jnp.float32)

    def one_patch(grad_ext, index):
        index = index.astype(jnp.int32)
        tile = (index // SLOTS).astype(jnp.int32)
        slot = (index % SLOTS).astype(jnp.int32)
        row = (tile * PATCH + places[index, 0]).astype(jnp.int32)
        column = places[index, 1].astype(jnp.int32)
        zero = jnp.zeros((), jnp.int32)
        window = lax.dynamic_slice(extended, (zero, zero, row, column), (SLICES, 2, PATCH, PATCH))
        live = (slot < live_counts[tile]).astype(jnp.float32)
        wave_now = start_wave
        saved = []
        for layer in range(SLICES):
            psi = propagate(wave_now, tables, True)
            saved.append(psi)
            wave_now = complex_product(psi, window[layer], False)
        chi_wave = far_field(wave_now, amplitude[index], live, tables)
        terms = [None] * SLICES
        for layer in range(SLICES - 1, -1, -1):
            terms[layer] = complex_product(saved[layer], chi_wave, True)
            if layer > 0:
                back = complex_product(window[layer], chi_wave, True)
                chi_wave = propagate(back, tables, False)
        stacked = jnp.stack(terms, axis=0)
        current = lax.dynamic_slice(grad_ext, (zero, zero, row, column), (SLICES, 2, PATCH, PATCH))
        updated = (current + stacked).astype(grad_ext.dtype)
        grad_ext = lax.dynamic_update_slice(grad_ext, updated, (zero, zero, row, column))
        return (grad_ext, None)
    grad_ext = jnp.zeros((SLICES, 2, ROWS + PATCH, WIDTH), jnp.float32)
    grad_ext, _ = lax.scan(one_patch, grad_ext, jnp.arange(tiles * SLOTS, dtype=jnp.int32))
    return grad_ext[:, :, :ROWS].at[:, :, :PATCH].add(grad_ext[:, :, ROWS:])
```

```python
import math

import jax
import jax.numpy as jnp
from jax import lax
from jax.sharding import PartitionSpec as P

chirp_rate = 0.25


def shifted(block, axis, distance):
    devices = range(lax.axis_size(axis))
    route = [((i - distance) % len(devices), i) for i in devices]
    return lax.ppermute(block, axis, route)


def passed_along(block, axis, distance):
    devices = range(lax.axis_size(axis))
    route = [(i - distance, i) for i in devices if i - distance in devices]
    return lax.ppermute(block, axis, route)


def make_tables(length):
    index = jnp.arange(length, dtype=jnp.int32)
    product = index[:, None] * index[None, :] % length
    angle = 2.0 * math.pi / length * product.astype(jnp.float32)
    factor = 1.0 / math.sqrt(length)
    table_real = jnp.cos(angle) * factor
    table_imag = -jnp.sin(angle) * factor
    freq = jnp.where(index < length // 2, index, index - length).astype(jnp.float32)
    theta = -math.pi * chirp_rate / length * (freq[:, None] ** 2 + freq[None, :] ** 2)
    return (table_real, table_imag, jnp.cos(theta), jnp.sin(theta))


def left_product(matrix, field):
    return jnp.einsum(
        "jk,...kl->...jl",
        matrix,
        field,
        preferred_element_type=jnp.float32,
        precision=lax.Precision.HIGHEST,
    )


def right_product(field, matrix):
    return jnp.einsum(
        "...jk,kl->...jl",
        field,
        matrix,
        preferred_element_type=jnp.float32,
        precision=lax.Precision.HIGHEST,
    )


def transform(field, tables, forward):
    table_real = tables[0]
    table_imag = tables[1] if forward else -tables[1]
    real_part = field[..., 0, :, :]
    imag_part = field[..., 1, :, :]
    first_real = left_product(table_real, real_part) - left_product(table_imag, imag_part)
    first_imag = left_product(table_real, imag_part) + left_product(table_imag, real_part)
    out_real = right_product(first_real, table_real) - right_product(first_imag, table_imag)
    out_imag = right_product(first_real, table_imag) + right_product(first_imag, table_real)
    return jnp.stack([out_real, out_imag], axis=-3)


def complex_product(first, second, conjugate):
    first_real = first[..., 0, :, :]
    first_imag = first[..., 1, :, :]
    if conjugate:
        first_imag = -first_imag
    second_real = second[..., 0, :, :]
    second_imag = second[..., 1, :, :]
    return jnp.stack(
        [
            first_real * second_real - first_imag * second_imag,
            first_real * second_imag + first_imag * second_real,
        ],
        axis=-3,
    )


def propagate(field, tables, forward):
    spectrum = transform(field, tables, True)
    sine = tables[3] if forward else -tables[3]
    chirp = jnp.stack([tables[2], sine], axis=0)
    return transform(complex_product(spectrum, chirp, False), tables, False)


def far_field(exit_wave, measured, live, tables):
    spectrum = transform(exit_wave, tables, True)
    power = spectrum[..., 0, :, :] ** 2 + spectrum[..., 1, :, :] ** 2
    keep = live[:, None, None] * (1.0 - measured / jnp.sqrt(power + 1.0))
    residual = spectrum * keep[..., None, :, :]
    return transform(residual, tables, False)


def forward_local(wave_in, windows, tables):
    saved = []
    for layer in range(windows.shape[1]):
        psi = propagate(wave_in, tables, True)
        saved.append(psi)
        wave_in = complex_product(psi, windows[:, layer], False)
    return (wave_in, jnp.stack(saved, axis=1))


def adjoint_local(chi_wave, windows, saved, tables):
    terms = [None] * windows.shape[1]
    for layer in range(windows.shape[1] - 1, -1, -1):
        terms[layer] = complex_product(saved[:, layer], chi_wave, True)
        back = complex_product(windows[:, layer], chi_wave, True)
        chi_wave = propagate(back, tables, False)
    return (chi_wave, jnp.stack(terms, axis=1))


def cut_columns(block, column, width):
    zero = jnp.zeros((), jnp.int32)
    start = (zero,) * (block.ndim - 1) + (column,)
    return lax.dynamic_slice(block, start, block.shape[:-1] + (width,))


def cut_rows(block, row, height):
    zero = jnp.zeros((), jnp.int32)
    start = (zero,) * (block.ndim - 2) + (row, zero)
    return lax.dynamic_slice(block, start, block.shape[:-2] + (height, block.shape[-1]))


def add_at_column(target, block, column):
    zero = jnp.zeros((), jnp.int32)
    start = (zero,) * (target.ndim - 1) + (column,)
    current = lax.dynamic_slice(target, start, block.shape)
    return lax.dynamic_update_slice(target, current + block, start)


def body(probe, slices, positions, counts, amplitude):
    patch = probe.shape[-1]
    slots = positions.shape[0]
    layers = slices.shape[0]
    tile_rows = slices.shape[2]
    tables = make_tables(patch)
    depth_index = lax.axis_index("depth")
    depth_count = lax.axis_size("depth")
    last_group = depth_count - 1
    before = shifted(positions, "scan", 1)

    def neighbour_part(layer):
        parts = [cut_columns(slices[layer, :, :patch], before[b, 1], patch) for b in range(slots)]
        return shifted(jnp.stack(parts, axis=0), "scan", -1)

    below = [neighbour_part(layer) for layer in range(layers)]

    def window(b, layer):
        own = cut_columns(slices[layer, :, :patch], positions[b, 1], patch)
        both = jnp.concatenate([own, below[layer][b]], axis=-2)
        return cut_rows(both, positions[b, 0], patch)

    live = (jnp.arange(slots, dtype=jnp.int32) < counts[0]).astype(jnp.float32)
    wave_shape = (slots, 2, patch, patch)

    def forward_stage(wave_in, first):
        saved = []
        for layer in range(layers):
            if first and layer == 0:
                psi = jnp.broadcast_to(propagate(probe[None], tables, True), wave_shape)
            else:
                psi = propagate(wave_in, tables, True)
            saved.append(psi)
            windows = jnp.stack([window(b, layer) for b in range(slots)], axis=0)
            wave_in = complex_product(psi, windows, False)
        return (wave_in, jnp.stack(saved, axis=1))

    def adjoint_stage(chi_wave, saved, first):
        terms = [None] * layers
        for layer in range(layers - 1, -1, -1):
            terms[layer] = complex_product(saved[:, layer], chi_wave, True)
            if first and layer == 0:
                continue
            windows = jnp.stack([window(b, layer) for b in range(slots)], axis=0)
            back = complex_product(windows, chi_wave, True)
            chi_wave = propagate(back, tables, False)
        return (chi_wave, jnp.stack(terms, axis=1))

    wave_now = jnp.zeros(wave_shape, jnp.float32)
    saved = jnp.zeros((slots, layers, 2, patch, patch), jnp.float32)
    for step_number in range(depth_count):

        def advance(state, first=step_number == 0):
            return forward_stage(state[0], first)

        def passing(state):
            return state

        wave_now, saved = lax.cond(depth_index == step_number, advance, passing, (wave_now, saved))
        if step_number < depth_count - 1:
            wave_now = passed_along(wave_now, "depth", 1)
    chi_wave = lax.cond(
        depth_index == last_group,
        lambda waves: far_field(waves, amplitude, live, tables),
        lambda waves: jnp.zeros(wave_shape, jnp.float32),
        wave_now,
    )
    terms = jnp.zeros((slots, layers, 2, patch, patch), jnp.float32)
    for step_number in range(depth_count - 1, -1, -1):

        def retreat(state, first=step_number == 0):
            return adjoint_stage(state[0], saved, first)

        def keeping(state):
            return state

        chi_wave, terms = lax.cond(depth_index == step_number, retreat, keeping, (chi_wave, terms))
        if step_number > 0:
            chi_wave = passed_along(chi_wave, "depth", -1)
    blank = jnp.zeros(terms.shape[:-2] + (patch, patch), jnp.float32)
    padded = jnp.concatenate([blank, terms, blank], axis=-2)
    upper = [cut_rows(padded[b], patch - positions[b, 0], patch) for b in range(slots)]
    lower = [cut_rows(padded[b], 2 * patch - positions[b, 0], patch) for b in range(slots)]
    arrived = shifted(jnp.stack(lower, axis=0), "scan", 1)
    gradient = jnp.zeros((layers, 2, tile_rows, slices.shape[3]), jnp.float32)
    for b in range(slots):
        gradient = add_at_column(gradient, upper[b], positions[b, 1])
    for b in range(slots):
        gradient = add_at_column(gradient, arrived[b], before[b, 1])
    return gradient


def solution(mesh):
    return jax.shard_map(
        body,
        mesh=mesh,
        in_specs=(
            P(),
            P("depth", None, ("groups", "scan"), None),
            P(("groups", "scan"), None),
            P(("groups", "scan")),
            P(("groups", "scan"), None, None),
        ),
        out_specs=P("depth", None, ("groups", "scan"), None),
        check_vma=False,
    )
```

```python
import math

import jax
import jax.numpy as jnp
from jax import lax
from jax.sharding import PartitionSpec as P

chirp_rate = 0.25


def shifted(block, axis, distance):
    devices = range(lax.axis_size(axis))
    route = [((i - distance) % len(devices), i) for i in devices]
    return lax.ppermute(block, axis, route)


def passed_along(block, axis, distance):
    devices = range(lax.axis_size(axis))
    route = [(i - distance, i) for i in devices if i - distance in devices]
    return lax.ppermute(block, axis, route)


def make_tables(length):
    index = jnp.arange(length, dtype=jnp.int32)
    product = index[:, None] * index[None, :] % length
    angle = 2.0 * math.pi / length * product.astype(jnp.float32)
    factor = 1.0 / math.sqrt(length)
    table_real = jnp.cos(angle) * factor
    table_imag = -jnp.sin(angle) * factor
    freq = jnp.where(index < length // 2, index, index - length).astype(jnp.float32)
    theta = -math.pi * chirp_rate / length * (freq[:, None] ** 2 + freq[None, :] ** 2)
    return (table_real, table_imag, jnp.cos(theta), jnp.sin(theta))


def left_product(matrix, field):
    return jnp.einsum(
        "jk,...kl->...jl",
        matrix,
        field,
        preferred_element_type=jnp.float32,
        precision=lax.Precision.HIGHEST,
    )


def right_product(field, matrix):
    return jnp.einsum(
        "...jk,kl->...jl",
        field,
        matrix,
        preferred_element_type=jnp.float32,
        precision=lax.Precision.HIGHEST,
    )


def transform(field, tables, forward):
    table_real = tables[0]
    table_imag = tables[1] if forward else -tables[1]
    real_part = field[..., 0, :, :]
    imag_part = field[..., 1, :, :]
    first_real = left_product(table_real, real_part) - left_product(table_imag, imag_part)
    first_imag = left_product(table_real, imag_part) + left_product(table_imag, real_part)
    out_real = right_product(first_real, table_real) - right_product(first_imag, table_imag)
    out_imag = right_product(first_real, table_imag) + right_product(first_imag, table_real)
    return jnp.stack([out_real, out_imag], axis=-3)


def complex_product(first, second, conjugate):
    first_real = first[..., 0, :, :]
    first_imag = first[..., 1, :, :]
    if conjugate:
        first_imag = -first_imag
    second_real = second[..., 0, :, :]
    second_imag = second[..., 1, :, :]
    return jnp.stack(
        [
            first_real * second_real - first_imag * second_imag,
            first_real * second_imag + first_imag * second_real,
        ],
        axis=-3,
    )


def propagate(field, tables, forward):
    spectrum = transform(field, tables, True)
    sine = tables[3] if forward else -tables[3]
    chirp = jnp.stack([tables[2], sine], axis=0)
    return transform(complex_product(spectrum, chirp, False), tables, False)


def far_field(exit_wave, measured, live, tables):
    spectrum = transform(exit_wave, tables, True)
    power = spectrum[..., 0, :, :] ** 2 + spectrum[..., 1, :, :] ** 2
    keep = live[:, None, None] * (1.0 - measured / jnp.sqrt(power + 1.0))
    residual = spectrum * keep[..., None, :, :]
    return transform(residual, tables, False)


def cut_columns(block, column, width):
    zero = jnp.zeros((), jnp.int32)
    start = (zero,) * (block.ndim - 1) + (column,)
    return lax.dynamic_slice(block, start, block.shape[:-1] + (width,))


def cut_rows(block, row, height):
    zero = jnp.zeros((), jnp.int32)
    start = (zero,) * (block.ndim - 2) + (row, zero)
    return lax.dynamic_slice(block, start, block.shape[:-2] + (height, block.shape[-1]))


def add_at_column(target, block, column):
    zero = jnp.zeros((), jnp.int32)
    start = (zero,) * (target.ndim - 1) + (column,)
    current = lax.dynamic_slice(target, start, block.shape)
    return lax.dynamic_update_slice(target, current + block, start)


def body(probe, slices, positions, counts, amplitude):
    patch = probe.shape[-1]
    slots = positions.shape[0]
    layers = slices.shape[0]
    tile_rows = slices.shape[2]
    tables = make_tables(patch)
    depth_index = lax.axis_index("depth")
    depth_count = lax.axis_size("depth")
    before = shifted(positions, "scan", 1)

    def windows_of(layer):
        parts = [cut_columns(slices[layer, :, :patch], before[b, 1], patch) for b in range(slots)]
        below = shifted(jnp.stack(parts, axis=0), "scan", -1)
        cut = []
        for b in range(slots):
            own = cut_columns(slices[layer, :, :patch], positions[b, 1], patch)
            both = jnp.concatenate([own, below[b]], axis=-2)
            cut.append(cut_rows(both, positions[b, 0], patch))
        return jnp.stack(cut, axis=0)

    windows = [windows_of(layer) for layer in range(layers)]
    live = (jnp.arange(slots, dtype=jnp.int32) < counts[0]).astype(jnp.float32)
    wave_shape = (slots, 2, patch, patch)

    first_psi = jnp.broadcast_to(propagate(probe[None], tables, True), wave_shape)
    wave_now = None
    saved = []
    for step_number in range(depth_count):
        psis = []
        for layer in range(layers):
            if step_number == 0 and layer == 0:
                psi = first_psi
            else:
                psi = propagate(wave_now, tables, True)
            psis.append(psi)
            wave_now = complex_product(psi, windows[layer], False)
        saved.append(psis)
        if step_number < depth_count - 1:
            wave_now = passed_along(wave_now, "depth", 1)
    chi_wave = far_field(wave_now, amplitude, live, tables)
    terms = [[None] * layers for _ in range(depth_count)]
    for step_number in range(depth_count - 1, -1, -1):
        for layer in range(layers - 1, -1, -1):
            terms[step_number][layer] = complex_product(saved[step_number][layer], chi_wave, True)
            if step_number == 0 and layer == 0:
                continue
            back = complex_product(windows[layer], chi_wave, True)
            chi_wave = propagate(back, tables, False)
        if step_number > 0:
            chi_wave = passed_along(chi_wave, "depth", -1)
    gradient = jnp.zeros((layers, 2, tile_rows, slices.shape[3]), jnp.float32)
    blank = jnp.zeros((2, patch, patch), jnp.float32)
    layer_grads = []
    for layer in range(layers - 1, -1, -1):
        mine = lax.select_n(depth_index, *[terms[k][layer] for k in range(depth_count)])
        upper = []
        lower = []
        for b in range(slots):
            padded = jnp.concatenate([blank, mine[b], blank], axis=-2)
            upper.append(cut_rows(padded, patch - positions[b, 0], patch))
            lower.append(cut_rows(padded, 2 * patch - positions[b, 0], patch))
        arrived = shifted(jnp.stack(lower, axis=0), "scan", 1)
        grad = jnp.zeros((2, tile_rows, slices.shape[3]), jnp.float32)
        for b in range(slots):
            grad = add_at_column(grad, upper[b], positions[b, 1])
        for b in range(slots):
            grad = add_at_column(grad, arrived[b], before[b, 1])
        layer_grads.append(grad)
    return jnp.stack(layer_grads[::-1], axis=0)


def solution(mesh):
    return jax.shard_map(
        body,
        mesh=mesh,
        in_specs=(
            P(),
            P("depth", None, ("groups", "scan"), None),
            P(("groups", "scan"), None),
            P(("groups", "scan")),
            P(("groups", "scan"), None, None),
        ),
        out_specs=P("depth", None, ("groups", "scan"), None),
        check_vma=False,
    )
```

```python
import math

import jax
import jax.numpy as jnp
from jax import lax
from jax.sharding import PartitionSpec as P

chirp_rate = 0.25


def shifted(block, axis, distance):
    devices = range(lax.axis_size(axis))
    route = [((i - distance) % len(devices), i) for i in devices]
    return lax.ppermute(block, axis, route)


def passed_along(block, axis, distance):
    devices = range(lax.axis_size(axis))
    route = [(i - distance, i) for i in devices if i - distance in devices]
    return lax.ppermute(block, axis, route)


def make_tables(length):
    index = jnp.arange(length, dtype=jnp.int32)
    product = index[:, None] * index[None, :] % length
    angle = 2.0 * math.pi / length * product.astype(jnp.float32)
    factor = 1.0 / math.sqrt(length)
    table_real = jnp.cos(angle) * factor
    table_imag = -jnp.sin(angle) * factor
    freq = jnp.where(index < length // 2, index, index - length).astype(jnp.float32)
    theta = -math.pi * chirp_rate / length * (freq[:, None] ** 2 + freq[None, :] ** 2)
    return (table_real, table_imag, jnp.cos(theta), jnp.sin(theta))


def left_product(matrix, field):
    return jnp.einsum(
        "jk,...kl->...jl",
        matrix,
        field,
        preferred_element_type=jnp.float32,
        precision=lax.Precision.HIGHEST,
    )


def right_product(field, matrix):
    return jnp.einsum(
        "...jk,kl->...jl",
        field,
        matrix,
        preferred_element_type=jnp.float32,
        precision=lax.Precision.HIGHEST,
    )


def transform(field, tables, forward):
    table_real = tables[0]
    table_imag = tables[1] if forward else -tables[1]
    real_part = field[..., 0, :, :]
    imag_part = field[..., 1, :, :]
    first_real = left_product(table_real, real_part) - left_product(table_imag, imag_part)
    first_imag = left_product(table_real, imag_part) + left_product(table_imag, real_part)
    out_real = right_product(first_real, table_real) - right_product(first_imag, table_imag)
    out_imag = right_product(first_real, table_imag) + right_product(first_imag, table_real)
    return jnp.stack([out_real, out_imag], axis=-3)


def complex_product(first, second, conjugate):
    first_real = first[..., 0, :, :]
    first_imag = first[..., 1, :, :]
    if conjugate:
        first_imag = -first_imag
    second_real = second[..., 0, :, :]
    second_imag = second[..., 1, :, :]
    return jnp.stack(
        [
            first_real * second_real - first_imag * second_imag,
            first_real * second_imag + first_imag * second_real,
        ],
        axis=-3,
    )


def propagate(field, tables, forward):
    spectrum = transform(field, tables, True)
    sine = tables[3] if forward else -tables[3]
    chirp = jnp.stack([tables[2], sine], axis=0)
    return transform(complex_product(spectrum, chirp, False), tables, False)


def far_field(exit_wave, measured, live, tables):
    spectrum = transform(exit_wave, tables, True)
    power = spectrum[..., 0, :, :] ** 2 + spectrum[..., 1, :, :] ** 2
    keep = live[:, None, None] * (1.0 - measured / jnp.sqrt(power + 1.0))
    residual = spectrum * keep[..., None, :, :]
    return transform(residual, tables, False)


def cut_columns(block, column, width):
    zero = jnp.zeros((), jnp.int32)
    start = (zero,) * (block.ndim - 1) + (column,)
    return lax.dynamic_slice(block, start, block.shape[:-1] + (width,))


def cut_rows(block, row, height):
    zero = jnp.zeros((), jnp.int32)
    start = (zero,) * (block.ndim - 2) + (row, zero)
    return lax.dynamic_slice(block, start, block.shape[:-2] + (height, block.shape[-1]))


def add_at_column(target, block, column):
    zero = jnp.zeros((), jnp.int32)
    start = (zero,) * (target.ndim - 1) + (column,)
    current = lax.dynamic_slice(target, start, block.shape)
    return lax.dynamic_update_slice(target, current + block, start)


def body(probe, slices, positions, counts, amplitude):
    patch = probe.shape[-1]
    slots = positions.shape[0]
    layers = slices.shape[0]
    tile_rows = slices.shape[2]
    tables = lax.optimization_barrier(make_tables(patch))
    depth_index = lax.axis_index("depth")
    depth_count = lax.axis_size("depth")
    before = shifted(positions, "scan", 1)

    def windows_of(layer):
        parts = [cut_columns(slices[layer, :, :patch], before[b, 1], patch) for b in range(slots)]
        below = shifted(jnp.stack(parts, axis=0), "scan", -1)
        cut = []
        for b in range(slots):
            own = cut_columns(slices[layer, :, :patch], positions[b, 1], patch)
            both = jnp.concatenate([own, below[b]], axis=-2)
            cut.append(cut_rows(both, positions[b, 0], patch))
        return jnp.stack(cut, axis=0)

    windows = [windows_of(layer) for layer in range(layers)]
    live = (jnp.arange(slots, dtype=jnp.int32) < counts[0]).astype(jnp.float32)
    wave_shape = (slots, 2, patch, patch)

    first_psi = jnp.broadcast_to(propagate(probe[None], tables, True), wave_shape)
    wave_now = None
    saved = []
    for step_number in range(depth_count):
        psis = []
        for layer in range(layers):
            if step_number == 0 and layer == 0:
                psi = first_psi
            else:
                psi = propagate(wave_now, tables, True)
            psis.append(psi)
            wave_now = complex_product(psi, windows[layer], False)
        saved.append(psis)
        if step_number < depth_count - 1:
            wave_now = passed_along(wave_now, "depth", 1)
    chi_wave = far_field(wave_now, amplitude, live, tables)
    terms = [[None] * layers for _ in range(depth_count)]
    for step_number in range(depth_count - 1, -1, -1):
        for layer in range(layers - 1, -1, -1):
            terms[step_number][layer] = complex_product(saved[step_number][layer], chi_wave, True)
            if step_number == 0 and layer == 0:
                continue
            back = complex_product(windows[layer], chi_wave, True)
            chi_wave = propagate(back, tables, False)
        if step_number > 0:
            chi_wave = passed_along(chi_wave, "depth", -1)
    gradient = jnp.zeros((layers, 2, tile_rows, slices.shape[3]), jnp.float32)
    blank = jnp.zeros((2, patch, patch), jnp.float32)
    layer_grads = []
    for layer in range(layers - 1, -1, -1):
        mine = lax.select_n(depth_index, *[terms[k][layer] for k in range(depth_count)])
        upper = []
        lower = []
        for b in range(slots):
            padded = jnp.concatenate([blank, mine[b], blank], axis=-2)
            upper.append(cut_rows(padded, patch - positions[b, 0], patch))
            lower.append(cut_rows(padded, 2 * patch - positions[b, 0], patch))
        arrived = shifted(jnp.stack(lower, axis=0), "scan", 1)
        grad = jnp.zeros((2, tile_rows, slices.shape[3]), jnp.float32)
        for b in range(slots):
            grad = add_at_column(grad, upper[b], positions[b, 1])
        for b in range(slots):
            grad = add_at_column(grad, arrived[b], before[b, 1])
        layer_grads.append(grad)
    return jnp.stack(layer_grads[::-1], axis=0)


def solution(mesh):
    return jax.shard_map(
        body,
        mesh=mesh,
        in_specs=(
            P(),
            P("depth", None, ("groups", "scan"), None),
            P(("groups", "scan"), None),
            P(("groups", "scan")),
            P(("groups", "scan"), None, None),
        ),
        out_specs=P("depth", None, ("groups", "scan"), None),
        check_vma=False,
    )
```

```python
import math

import jax
import jax.numpy as jnp
from jax import lax
from jax.sharding import PartitionSpec as P

chirp_rate = 0.25


def shifted(block, axis, distance):
    devices = range(lax.axis_size(axis))
    route = [((i - distance) % len(devices), i) for i in devices]
    return lax.ppermute(block, axis, route)


def passed_along(block, axis, distance):
    devices = range(lax.axis_size(axis))
    route = [(i - distance, i) for i in devices if i - distance in devices]
    return lax.ppermute(block, axis, route)


def make_tables(length):
    index = jnp.arange(length, dtype=jnp.int32)
    product = index[:, None] * index[None, :] % length
    angle = 2.0 * math.pi / length * product.astype(jnp.float32)
    factor = 1.0 / math.sqrt(length)
    table_real = jnp.cos(angle) * factor
    table_imag = -jnp.sin(angle) * factor
    freq = jnp.where(index < length // 2, index, index - length).astype(jnp.float32)
    theta = -math.pi * chirp_rate / length * (freq[:, None] ** 2 + freq[None, :] ** 2)
    return (table_real, table_imag, jnp.cos(theta), jnp.sin(theta))


def left_product(matrix, field):
    return jnp.einsum(
        "jk,...kl->...jl",
        matrix,
        field,
        preferred_element_type=jnp.float32,
        precision=lax.Precision.HIGHEST,
    )


def right_product(field, matrix):
    return jnp.einsum(
        "...jk,kl->...jl",
        field,
        matrix,
        preferred_element_type=jnp.float32,
        precision=lax.Precision.HIGHEST,
    )


def transform(field, tables, forward):
    table_real = tables[0]
    table_imag = tables[1] if forward else -tables[1]
    real_part = field[..., 0, :, :]
    imag_part = field[..., 1, :, :]
    first_real = left_product(table_real, real_part) - left_product(table_imag, imag_part)
    first_imag = left_product(table_real, imag_part) + left_product(table_imag, real_part)
    out_real = right_product(first_real, table_real) - right_product(first_imag, table_imag)
    out_imag = right_product(first_real, table_imag) + right_product(first_imag, table_real)
    return jnp.stack([out_real, out_imag], axis=-3)


def complex_product(first, second, conjugate):
    first_real = first[..., 0, :, :]
    first_imag = first[..., 1, :, :]
    if conjugate:
        first_imag = -first_imag
    second_real = second[..., 0, :, :]
    second_imag = second[..., 1, :, :]
    return jnp.stack(
        [
            first_real * second_real - first_imag * second_imag,
            first_real * second_imag + first_imag * second_real,
        ],
        axis=-3,
    )


def propagate(field, tables, forward):
    spectrum = transform(field, tables, True)
    sine = tables[3] if forward else -tables[3]
    chirp = jnp.stack([tables[2], sine], axis=0)
    return transform(complex_product(spectrum, chirp, False), tables, False)


def far_field(exit_wave, measured, live, tables):
    spectrum = transform(exit_wave, tables, True)
    power = spectrum[..., 0, :, :] ** 2 + spectrum[..., 1, :, :] ** 2
    keep = live[:, None, None] * (1.0 - measured / jnp.sqrt(power + 1.0))
    residual = spectrum * keep[..., None, :, :]
    return transform(residual, tables, False)


def cut_columns(block, column, width):
    zero = jnp.zeros((), jnp.int32)
    start = (zero,) * (block.ndim - 1) + (column,)
    return lax.dynamic_slice(block, start, block.shape[:-1] + (width,))


def cut_rows(block, row, height):
    zero = jnp.zeros((), jnp.int32)
    start = (zero,) * (block.ndim - 2) + (row, zero)
    return lax.dynamic_slice(block, start, block.shape[:-2] + (height, block.shape[-1]))


def place_columns(block, column, width):
    pad = [(0, 0)] * (block.ndim - 1) + [(width, width - block.shape[-1])]
    return cut_columns(jnp.pad(block, pad), width - column, width)


def pick(stack, index):
    return lax.dynamic_index_in_dim(stack, index, 0, keepdims=False)


def body(probe, slices, positions, counts, amplitude):
    patch = probe.shape[-1]
    slots = positions.shape[0]
    layers = slices.shape[0]
    tile_rows = slices.shape[2]
    width = slices.shape[3]
    tables = lax.optimization_barrier(make_tables(patch))
    depth_index = lax.axis_index("depth")
    depth_count = lax.axis_size("depth")
    last_group = depth_count - 1
    steps = slots + depth_count - 1
    before = shifted(positions, "scan", 1)
    own_rows = slices[:, :, :patch]

    windows = []
    for b in range(slots):
        below = shifted(cut_columns(own_rows, before[b, 1], patch), "scan", -1)
        own = cut_columns(own_rows, positions[b, 1], patch)
        both = jnp.concatenate([own, below], axis=-2)
        windows.append(cut_rows(both, positions[b, 0], patch))
    windows = jnp.stack(windows, axis=0)
    live = (jnp.arange(slots, dtype=jnp.int32) < counts[0]).astype(jnp.float32)

    first_psi = propagate(probe[None], tables, True)[0]
    wave_now = None
    saved = []
    exits = []
    for step_number in range(steps):
        slot = jnp.clip(step_number - depth_index, 0, slots - 1)
        mine = pick(windows, slot)
        psis = []
        for layer in range(layers):
            if layer == 0 and step_number == 0:
                psi = first_psi
            elif layer == 0:
                psi = jnp.where(depth_index == 0, first_psi, propagate(wave_now, tables, True))
            else:
                psi = propagate(wave_now, tables, True)
            psis.append(psi)
            wave_now = complex_product(psi, mine[layer], False)
        saved.append(jnp.stack(psis, axis=0))
        if step_number >= last_group:
            exits.append(wave_now)
        if step_number < steps - 1:
            wave_now = passed_along(wave_now, "depth", 1)
    saved = jnp.stack(saved, axis=0)
    chi_far = far_field(jnp.stack(exits, axis=0), amplitude, live, tables)

    chi_wave = None
    terms = []
    for step_number in range(steps):
        slot = jnp.clip(step_number - last_group + depth_index, 0, slots - 1)
        mine = pick(windows, slot)
        psis = pick(saved, jnp.clip(step_number - last_group + 2 * depth_index, 0, steps - 1))
        start = chi_far[min(step_number, slots - 1)]
        chi_wave = start if chi_wave is None else jnp.where(depth_index == last_group, start, chi_wave)
        found = [None] * layers
        for layer in range(layers - 1, -1, -1):
            found[layer] = complex_product(psis[layer], chi_wave, True)
            if layer == 0 and step_number == steps - 1:
                continue
            back = complex_product(mine[layer], chi_wave, True)
            chi_wave = propagate(back, tables, False)
        terms.append(jnp.stack(found, axis=0))
        if step_number < steps - 1:
            chi_wave = passed_along(chi_wave, "depth", -1)
    terms = jnp.stack(terms, axis=0)

    blank = jnp.zeros((layers, 2, patch, patch), jnp.float32)
    gradient = jnp.zeros((layers, 2, tile_rows, width), jnp.float32)
    for b in range(slots):
        found = pick(terms, b + last_group - depth_index)
        padded = jnp.concatenate([blank, found, blank], axis=-2)
        upper = cut_rows(padded, patch - positions[b, 0], patch)
        lower = cut_rows(padded, 2 * patch - positions[b, 0], patch)
        arrived = shifted(lower, "scan", 1)
        gradient = gradient + place_columns(upper, positions[b, 1], width)
        gradient = gradient + place_columns(arrived, before[b, 1], width)
    return gradient


def solution(mesh):
    return jax.shard_map(
        body,
        mesh=mesh,
        in_specs=(
            P(),
            P("depth", None, ("groups", "scan"), None),
            P(("groups", "scan"), None),
            P(("groups", "scan")),
            P(("groups", "scan"), None, None),
        ),
        out_specs=P("depth", None, ("groups", "scan"), None),
        check_vma=False,
    )
```

```python
import math

import jax
import jax.numpy as jnp
from jax import lax
from jax.sharding import PartitionSpec as P

chirp_rate = 0.25


def shifted(block, axis, distance):
    devices = range(lax.axis_size(axis))
    route = [((i - distance) % len(devices), i) for i in devices]
    return lax.ppermute(block, axis, route)


def passed_along(block, axis, distance):
    devices = range(lax.axis_size(axis))
    route = [(i - distance, i) for i in devices if i - distance in devices]
    return lax.ppermute(block, axis, route)


def make_tables(length):
    index = jnp.arange(length, dtype=jnp.int32)
    product = index[:, None] * index[None, :] % length
    angle = 2.0 * math.pi / length * product.astype(jnp.float32)
    factor = 1.0 / math.sqrt(length)
    table_real = jnp.cos(angle) * factor
    table_imag = -jnp.sin(angle) * factor
    freq = jnp.where(index < length // 2, index, index - length).astype(jnp.float32)
    theta = -math.pi * chirp_rate / length * (freq[:, None] ** 2 + freq[None, :] ** 2)
    return (table_real, table_imag, jnp.cos(theta), jnp.sin(theta))


def left_product(matrix, field):
    return jnp.einsum(
        "jk,...kl->...jl",
        matrix,
        field,
        preferred_element_type=jnp.float32,
        precision=lax.Precision.HIGHEST,
    )


def right_product(field, matrix):
    return jnp.einsum(
        "...jk,kl->...jl",
        field,
        matrix,
        preferred_element_type=jnp.float32,
        precision=lax.Precision.HIGHEST,
    )


def transform(field, tables, forward):
    table_real = tables[0]
    table_imag = tables[1] if forward else -tables[1]
    real_part = field[..., 0, :, :]
    imag_part = field[..., 1, :, :]
    first_real = left_product(table_real, real_part) - left_product(table_imag, imag_part)
    first_imag = left_product(table_real, imag_part) + left_product(table_imag, real_part)
    out_real = right_product(first_real, table_real) - right_product(first_imag, table_imag)
    out_imag = right_product(first_real, table_imag) + right_product(first_imag, table_real)
    return jnp.stack([out_real, out_imag], axis=-3)


def complex_product(first, second, conjugate):
    first_real = first[..., 0, :, :]
    first_imag = first[..., 1, :, :]
    if conjugate:
        first_imag = -first_imag
    second_real = second[..., 0, :, :]
    second_imag = second[..., 1, :, :]
    return jnp.stack(
        [
            first_real * second_real - first_imag * second_imag,
            first_real * second_imag + first_imag * second_real,
        ],
        axis=-3,
    )


def propagate(field, tables, forward):
    spectrum = transform(field, tables, True)
    sine = tables[3] if forward else -tables[3]
    chirp = jnp.stack([tables[2], sine], axis=0)
    return transform(complex_product(spectrum, chirp, False), tables, False)


def far_field(exit_wave, measured, live, tables):
    spectrum = transform(exit_wave, tables, True)
    power = spectrum[..., 0, :, :] ** 2 + spectrum[..., 1, :, :] ** 2
    keep = live[:, None, None] * (1.0 - measured / jnp.sqrt(power + 1.0))
    residual = spectrum * keep[..., None, :, :]
    return transform(residual, tables, False)


def cut_columns(block, column, width):
    zero = jnp.zeros((), jnp.int32)
    start = (zero,) * (block.ndim - 1) + (column,)
    return lax.dynamic_slice(block, start, block.shape[:-1] + (width,))


def cut_rows(block, row, height):
    zero = jnp.zeros((), jnp.int32)
    start = (zero,) * (block.ndim - 2) + (row, zero)
    return lax.dynamic_slice(block, start, block.shape[:-2] + (height, block.shape[-1]))


def place_columns(block, column, width):
    pad = [(0, 0)] * (block.ndim - 1) + [(width, width - block.shape[-1])]
    return cut_columns(jnp.pad(block, pad), width - column, width)


def pick(stack, index):
    return lax.dynamic_index_in_dim(stack, index, 0, keepdims=False)


def body(probe, slices, positions, counts, amplitude):
    patch = probe.shape[-1]
    slots = positions.shape[0]
    layers = slices.shape[0]
    tile_rows = slices.shape[2]
    width = slices.shape[3]
    tables = lax.optimization_barrier(make_tables(patch))
    depth_index = lax.axis_index("depth")
    depth_count = lax.axis_size("depth")
    last_group = depth_count - 1
    steps = slots + depth_count - 1
    before = shifted(positions, "scan", 1)
    own_rows = slices[:, :, :patch]

    windows = [[None] * layers for _ in range(slots)]
    previous = None
    for b in range(slots):
        for layer in range(layers):
            piece = cut_columns(own_rows[layer], before[b, 1], patch)
            if previous is None:
                probe, piece = lax.optimization_barrier((probe, piece))
            else:
                piece, previous = lax.optimization_barrier((piece, previous))
            below = shifted(piece, "scan", -1)
            previous = below
            own = cut_columns(own_rows[layer], positions[b, 1], patch)
            windows[b][layer] = cut_rows(jnp.concatenate([own, below], axis=-2), positions[b, 0], patch)
    live = (jnp.arange(slots, dtype=jnp.int32) < counts[0]).astype(jnp.float32)

    def window_at(step_number, slot, layer):
        reachable = min(step_number, slots - 1) + 1
        if reachable == 1:
            return windows[0][layer]
        stack = jnp.stack([windows[b][layer] for b in range(reachable)], axis=0)
        return pick(stack, jnp.clip(slot, 0, reachable - 1))

    first_psi = propagate(probe[None], tables, True)[0]
    wave_now = None
    saved = []
    exits = []
    for step_number in range(steps):
        slot = step_number - depth_index
        psis = []
        for layer in range(layers):
            if layer == 0 and step_number == 0:
                psi = first_psi
            elif layer == 0:
                psi = jnp.where(depth_index == 0, first_psi, propagate(wave_now, tables, True))
            else:
                psi = propagate(wave_now, tables, True)
            psis.append(psi)
            wave_now = complex_product(psi, window_at(step_number, slot, layer), False)
        saved.append(jnp.stack(psis, axis=0))
        if step_number >= last_group:
            exits.append(wave_now)
        if step_number < steps - 1:
            wave_now = passed_along(wave_now, "depth", 1)
    saved = jnp.stack(saved, axis=0)
    chi_far = far_field(jnp.stack(exits, axis=0), amplitude, live, tables)

    chi_wave = None
    terms = []
    for step_number in range(steps):
        slot = step_number - last_group + depth_index
        psis = pick(saved, jnp.clip(step_number - last_group + 2 * depth_index, 0, steps - 1))
        start = chi_far[min(step_number, slots - 1)]
        chi_wave = start if chi_wave is None else jnp.where(depth_index == last_group, start, chi_wave)
        found = [None] * layers
        for layer in range(layers - 1, -1, -1):
            found[layer] = complex_product(psis[layer], chi_wave, True)
            if layer == 0 and step_number == steps - 1:
                continue
            back = complex_product(window_at(steps - 1, slot, layer), chi_wave, True)
            chi_wave = propagate(back, tables, False)
        terms.append(found)
        if step_number < steps - 1:
            chi_wave = passed_along(chi_wave, "depth", -1)

    blank = jnp.zeros((2, patch, patch), jnp.float32)
    gradient = [jnp.zeros((2, tile_rows, width), jnp.float32) for _ in range(layers)]
    for b in range(slots):
        for layer in range(layers - 1, -1, -1):
            stack = jnp.stack([terms[s][layer] for s in range(b, b + depth_count)], axis=0)
            found = pick(stack, last_group - depth_index)
            padded = jnp.concatenate([blank, found, blank], axis=-2)
            upper = cut_rows(padded, patch - positions[b, 0], patch)
            lower = cut_rows(padded, 2 * patch - positions[b, 0], patch)
            arrived = shifted(lower, "scan", 1)
            gradient[layer] = gradient[layer] + place_columns(upper, positions[b, 1], width)
            gradient[layer] = gradient[layer] + place_columns(arrived, before[b, 1], width)
    return jnp.stack(gradient, axis=0)


def solution(mesh):
    return jax.shard_map(
        body,
        mesh=mesh,
        in_specs=(
            P(),
            P("depth", None, ("groups", "scan"), None),
            P(("groups", "scan"), None),
            P(("groups", "scan")),
            P(("groups", "scan"), None, None),
        ),
        out_specs=P("depth", None, ("groups", "scan"), None),
        check_vma=False,
    )
```

```python
import math

import jax
import jax.numpy as jnp
from jax import lax
from jax.sharding import PartitionSpec as P

chirp_rate = 0.25


def shifted(block, axis, distance):
    devices = range(lax.axis_size(axis))
    route = [((i - distance) % len(devices), i) for i in devices]
    return lax.ppermute(block, axis, route)


def passed_along(block, axis, distance):
    devices = range(lax.axis_size(axis))
    route = [(i - distance, i) for i in devices if i - distance in devices]
    return lax.ppermute(block, axis, route)


def make_tables(length):
    index = jnp.arange(length, dtype=jnp.int32)
    product = index[:, None] * index[None, :] % length
    angle = 2.0 * math.pi / length * product.astype(jnp.float32)
    factor = 1.0 / math.sqrt(length)
    table_real = jnp.cos(angle) * factor
    table_imag = -jnp.sin(angle) * factor
    freq = jnp.where(index < length // 2, index, index - length).astype(jnp.float32)
    theta = -math.pi * chirp_rate / length * (freq[:, None] ** 2 + freq[None, :] ** 2)
    return (table_real, table_imag, jnp.cos(theta), jnp.sin(theta))


def left_product(matrix, field):
    return jnp.einsum(
        "jk,...kl->...jl",
        matrix,
        field,
        preferred_element_type=jnp.float32,
        precision=lax.Precision.HIGHEST,
    )


def right_product(field, matrix):
    return jnp.einsum(
        "...jk,kl->...jl",
        field,
        matrix,
        preferred_element_type=jnp.float32,
        precision=lax.Precision.HIGHEST,
    )


def transform(field, tables, forward):
    table_real = tables[0]
    table_imag = tables[1] if forward else -tables[1]
    real_part = field[..., 0, :, :]
    imag_part = field[..., 1, :, :]
    first_real = left_product(table_real, real_part) - left_product(table_imag, imag_part)
    first_imag = left_product(table_real, imag_part) + left_product(table_imag, real_part)
    out_real = right_product(first_real, table_real) - right_product(first_imag, table_imag)
    out_imag = right_product(first_real, table_imag) + right_product(first_imag, table_real)
    return jnp.stack([out_real, out_imag], axis=-3)


def complex_product(first, second, conjugate):
    first_real = first[..., 0, :, :]
    first_imag = first[..., 1, :, :]
    if conjugate:
        first_imag = -first_imag
    second_real = second[..., 0, :, :]
    second_imag = second[..., 1, :, :]
    return jnp.stack(
        [
            first_real * second_real - first_imag * second_imag,
            first_real * second_imag + first_imag * second_real,
        ],
        axis=-3,
    )


def propagate(field, tables, forward):
    spectrum = transform(field, tables, True)
    sine = tables[3] if forward else -tables[3]
    chirp = jnp.stack([tables[2], sine], axis=0)
    return transform(complex_product(spectrum, chirp, False), tables, False)


def far_field(exit_wave, measured, live, tables):
    spectrum = transform(exit_wave, tables, True)
    power = spectrum[..., 0, :, :] ** 2 + spectrum[..., 1, :, :] ** 2
    keep = live[:, None, None] * (1.0 - measured / jnp.sqrt(power + 1.0))
    residual = spectrum * keep[..., None, :, :]
    return transform(residual, tables, False)


def cut_columns(block, column, width):
    zero = jnp.zeros((), jnp.int32)
    start = (zero,) * (block.ndim - 1) + (column,)
    return lax.dynamic_slice(block, start, block.shape[:-1] + (width,))


def cut_rows(block, row, height):
    zero = jnp.zeros((), jnp.int32)
    start = (zero,) * (block.ndim - 2) + (row, zero)
    return lax.dynamic_slice(block, start, block.shape[:-2] + (height, block.shape[-1]))


def place_columns(block, column, width):
    pad = [(0, 0)] * (block.ndim - 1) + [(width, width - block.shape[-1])]
    return cut_columns(jnp.pad(block, pad), width - column, width)


def pick(stack, index):
    return lax.dynamic_index_in_dim(stack, index, 0, keepdims=False)


def swapped(block, axis):
    return lax.ppermute(block, axis, [(i, i ^ 1) for i in range(lax.axis_size(axis))])


def body(probe, slices, positions, counts, amplitude):
    patch = probe.shape[-1]
    slots = positions.shape[0]
    layers = slices.shape[0]
    tile_rows = slices.shape[2]
    width = slices.shape[3]
    tables = lax.optimization_barrier(make_tables(patch))
    depth_index = lax.axis_index("depth")
    depth_count = lax.axis_size("depth")
    assert slots == 2 and depth_count % 2 == 0
    pairs = depth_count // 2
    pair = depth_index // 2
    member = depth_index % 2
    span = 2 * layers
    before = shifted(positions, "scan", 1)
    own_rows = slices[:, :, :patch]

    windows = [[None] * layers for _ in range(slots)]
    previous = None
    for layer in range(layers):
        for b in (1, 0):
            piece = cut_columns(own_rows[layer], before[b, 1], patch)
            if previous is None:
                probe, piece = lax.optimization_barrier((probe, piece))
            else:
                piece, previous = lax.optimization_barrier((piece, previous))
            below = shifted(piece, "scan", -1)
            previous = below
            own = cut_columns(own_rows[layer], positions[b, 1], patch)
            windows[b][layer] = cut_rows(jnp.concatenate([own, below], axis=-2), positions[b, 0], patch)
    partner_windows = [
        swapped(jnp.where(member == 0, windows[1][layer], windows[0][layer]), "depth") for layer in range(layers)
    ]
    mine_windows = [jnp.where(member == 0, windows[0][layer], windows[1][layer]) for layer in range(layers)]
    path = []
    for j in range(span):
        first_half = j < layers
        path.append(
            jnp.where(
                member == (0 if first_half else 1),
                mine_windows[j % layers],
                partner_windows[j % layers],
            )
        )
    live = (jnp.arange(slots, dtype=jnp.int32) < counts[0]).astype(jnp.float32)
    my_live = jnp.where(member == 0, live[0], live[1])[None]
    my_amplitude = jnp.where(member == 0, amplitude[0], amplitude[1])[None]

    first_psi = propagate(probe[None], tables, True)[0]
    wave_now = None
    saved = []
    for step_number in range(pairs):
        psis = []
        for j in range(span):
            if j == 0 and step_number == 0:
                psi = first_psi
            else:
                psi = propagate(wave_now, tables, True)
            psis.append(psi)
            wave_now = complex_product(psi, path[j], False)
        saved.append(psis)
        if step_number < pairs - 1:
            wave_now = passed_along(wave_now, "depth", 2)
    chi_wave = far_field(wave_now[None], my_amplitude, my_live, tables)[0]

    terms = [None] * pairs
    for step_number in range(pairs - 1, -1, -1):
        found = [None] * span
        for j in range(span - 1, -1, -1):
            found[j] = complex_product(saved[step_number][j], chi_wave, True)
            if j == 0 and step_number == 0:
                continue
            back = complex_product(path[j], chi_wave, True)
            chi_wave = propagate(back, tables, False)
        terms[step_number] = found
        if step_number > 0:
            chi_wave = passed_along(chi_wave, "depth", -2)

    def my_terms(j):
        if pairs == 1:
            return terms[0][j]
        return pick(jnp.stack([terms[k][j] for k in range(pairs)], axis=0), pair)

    slot_terms = [[None] * layers for _ in range(slots)]
    for layer in range(layers - 1, -1, -1):
        kept = jnp.where(member == 0, my_terms(layer), my_terms(layers + layer))
        given = swapped(jnp.where(member == 0, my_terms(layers + layer), my_terms(layer)), "depth")
        slot_terms[0][layer] = jnp.where(member == 0, kept, given)
        slot_terms[1][layer] = jnp.where(member == 0, given, kept)

    blank = jnp.zeros((2, patch, patch), jnp.float32)
    gradient = [jnp.zeros((2, tile_rows, width), jnp.float32) for _ in range(layers)]
    for layer in range(layers - 1, -1, -1):
        for b in range(slots):
            padded = jnp.concatenate([blank, slot_terms[b][layer], blank], axis=-2)
            upper = cut_rows(padded, patch - positions[b, 0], patch)
            lower = cut_rows(padded, 2 * patch - positions[b, 0], patch)
            arrived = shifted(lower, "scan", 1)
            gradient[layer] = gradient[layer] + place_columns(upper, positions[b, 1], width)
            gradient[layer] = gradient[layer] + place_columns(arrived, before[b, 1], width)
    return jnp.stack(gradient, axis=0)


def solution(mesh):
    return jax.shard_map(
        body,
        mesh=mesh,
        in_specs=(
            P(),
            P("depth", None, ("groups", "scan"), None),
            P(("groups", "scan"), None),
            P(("groups", "scan")),
            P(("groups", "scan"), None, None),
        ),
        out_specs=P("depth", None, ("groups", "scan"), None),
        check_vma=False,
    )
```

```python
import math

import jax
import jax.numpy as jnp
from jax import lax
from jax.sharding import PartitionSpec as P

chirp_rate = 0.25


def shifted(block, axis, distance):
    devices = range(lax.axis_size(axis))
    route = [((i - distance) % len(devices), i) for i in devices]
    return lax.ppermute(block, axis, route)


def passed_along(block, axis, distance):
    devices = range(lax.axis_size(axis))
    route = [(i - distance, i) for i in devices if i - distance in devices]
    return lax.ppermute(block, axis, route)


def make_tables(length):
    index = jnp.arange(length, dtype=jnp.int32)
    product = index[:, None] * index[None, :] % length
    angle = 2.0 * math.pi / length * product.astype(jnp.float32)
    factor = 1.0 / math.sqrt(length)
    table_real = jnp.cos(angle) * factor
    table_imag = -jnp.sin(angle) * factor
    freq = jnp.where(index < length // 2, index, index - length).astype(jnp.float32)
    theta = -math.pi * chirp_rate / length * (freq[:, None] ** 2 + freq[None, :] ** 2)
    return (table_real, table_imag, jnp.cos(theta), jnp.sin(theta))


def left_product(matrix, field):
    return jnp.einsum(
        "jk,...kl->...jl",
        matrix,
        field,
        preferred_element_type=jnp.float32,
        precision=lax.Precision.HIGHEST,
    )


def right_product(field, matrix):
    return jnp.einsum(
        "...jk,kl->...jl",
        field,
        matrix,
        preferred_element_type=jnp.float32,
        precision=lax.Precision.HIGHEST,
    )


def transform(field, tables, forward):
    table_real = tables[0]
    table_imag = tables[1] if forward else -tables[1]
    real_part = field[..., 0, :, :]
    imag_part = field[..., 1, :, :]
    first_real = left_product(table_real, real_part) - left_product(table_imag, imag_part)
    first_imag = left_product(table_real, imag_part) + left_product(table_imag, real_part)
    out_real = right_product(first_real, table_real) - right_product(first_imag, table_imag)
    out_imag = right_product(first_real, table_imag) + right_product(first_imag, table_real)
    return jnp.stack([out_real, out_imag], axis=-3)


def complex_product(first, second, conjugate):
    first_real = first[..., 0, :, :]
    first_imag = first[..., 1, :, :]
    if conjugate:
        first_imag = -first_imag
    second_real = second[..., 0, :, :]
    second_imag = second[..., 1, :, :]
    return jnp.stack(
        [
            first_real * second_real - first_imag * second_imag,
            first_real * second_imag + first_imag * second_real,
        ],
        axis=-3,
    )


def propagate(field, tables, forward):
    spectrum = transform(field, tables, True)
    sine = tables[3] if forward else -tables[3]
    chirp = jnp.stack([tables[2], sine], axis=0)
    return transform(complex_product(spectrum, chirp, False), tables, False)


def far_field(exit_wave, measured, live, tables):
    spectrum = transform(exit_wave, tables, True)
    power = spectrum[..., 0, :, :] ** 2 + spectrum[..., 1, :, :] ** 2
    keep = live[:, None, None] * (1.0 - measured / jnp.sqrt(power + 1.0))
    residual = spectrum * keep[..., None, :, :]
    return transform(residual, tables, False)


def cut_columns(block, column, width):
    zero = jnp.zeros((), jnp.int32)
    start = (zero,) * (block.ndim - 1) + (column,)
    return lax.dynamic_slice(block, start, block.shape[:-1] + (width,))


def cut_rows(block, row, height):
    zero = jnp.zeros((), jnp.int32)
    start = (zero,) * (block.ndim - 2) + (row, zero)
    return lax.dynamic_slice(block, start, block.shape[:-2] + (height, block.shape[-1]))


def place_columns(block, column, width):
    pad = [(0, 0)] * (block.ndim - 1) + [(width, width - block.shape[-1])]
    return cut_columns(jnp.pad(block, pad), width - column, width)


def pick(stack, index):
    return lax.dynamic_index_in_dim(stack, index, 0, keepdims=False)


def swapped(block, axis):
    return lax.ppermute(block, axis, [(i, i ^ 1) for i in range(lax.axis_size(axis))])


def routed(block, destination):
    tiles = lax.axis_size("scan")
    groups = lax.axis_size("depth")
    route = []
    for t in range(tiles):
        for d in range(groups):
            target = destination(t, d)
            if target is not None:
                route.append((t * groups + d, (target[0] % tiles) * groups + target[1]))
    return lax.ppermute(block, ("scan", "depth"), route)


def body(probe, slices, positions, counts, amplitude):
    patch = probe.shape[-1]
    slots = positions.shape[0]
    layers = slices.shape[0]
    tile_rows = slices.shape[2]
    width = slices.shape[3]
    tables = lax.optimization_barrier(make_tables(patch))
    depth_index = lax.axis_index("depth")
    depth_count = lax.axis_size("depth")
    assert slots == 2 and depth_count % 2 == 0
    pairs = depth_count // 2
    pair = depth_index // 2
    member = depth_index % 2
    span = 2 * layers
    before = shifted(positions, "scan", 1)
    own_rows = slices[:, :, :patch]
    my_row = jnp.where(member == 0, positions[0, 0], positions[1, 0])
    my_column = jnp.where(member == 0, positions[0, 1], positions[1, 1])
    other_column = jnp.where(member == 0, positions[1, 1], positions[0, 1])

    swapped_rows = [swapped(cut_columns(own_rows[layer], other_column, patch), "depth") for layer in range(layers)]
    below = [None] * span
    previous = None
    for source in range(2):
        for layer in range(layers):
            got = []
            for b in range(slots):
                piece = cut_columns(own_rows[layer], before[b, 1], patch)
                if previous is None:
                    probe, piece = lax.optimization_barrier((probe, piece))
                else:
                    piece, previous = lax.optimization_barrier((piece, previous))
                got.append(
                    routed(
                        piece,
                        lambda t, d, b=b, source=source: (t - 1, d - source + b) if d % 2 == source else None,
                    )
                )
            previous = got[0] + got[1]
            below[source * layers + layer] = previous
    path = []
    for j in range(span):
        source = j // layers
        own = cut_columns(own_rows[j % layers], my_column, patch)
        own = jnp.where(member == source, own, swapped_rows[j % layers])
        path.append(cut_rows(jnp.concatenate([own, below[j]], axis=-2), my_row, patch))
    live = (jnp.arange(slots, dtype=jnp.int32) < counts[0]).astype(jnp.float32)
    my_live = jnp.where(member == 0, live[0], live[1])[None]
    my_amplitude = jnp.where(member == 0, amplitude[0], amplitude[1])[None]

    first_psi = propagate(probe[None], tables, True)[0]
    wave_now = None
    saved = []
    for step_number in range(pairs):
        psis = []
        for j in range(span):
            if j == 0 and step_number == 0:
                psi = first_psi
            else:
                psi = propagate(wave_now, tables, True)
            psis.append(psi)
            wave_now = complex_product(psi, path[j], False)
        saved.append(psis)
        if step_number < pairs - 1:
            wave_now = passed_along(wave_now, "depth", 2)
    chi_wave = far_field(wave_now[None], my_amplitude, my_live, tables)[0]

    terms = [None] * pairs
    for step_number in range(pairs - 1, -1, -1):
        found = [None] * span
        for j in range(span - 1, -1, -1):
            found[j] = complex_product(saved[step_number][j], chi_wave, True)
            if j == 0 and step_number == 0:
                continue
            back = complex_product(path[j], chi_wave, True)
            chi_wave = propagate(back, tables, False)
        terms[step_number] = found
        if step_number > 0:
            chi_wave = passed_along(chi_wave, "depth", -2)

    blank = jnp.zeros((2, patch, patch), jnp.float32)
    uppers = [None] * span
    lowers = [[None] * 2 for _ in range(span)]
    swapped_upper = [None] * span
    for j in range(span - 1, -1, -1):
        if pairs == 1:
            mine = terms[0][j]
        else:
            mine = pick(jnp.stack([terms[k][j] for k in range(pairs)], axis=0), pair)
        padded = jnp.concatenate([blank, mine, blank], axis=-2)
        uppers[j] = cut_rows(padded, patch - my_row, patch)
        lower = cut_rows(padded, 2 * patch - my_row, patch)
        owner = j // layers
        for b in range(2):
            lowers[j][b] = routed(
                lower, lambda t, d, b=b, owner=owner: (t + 1, d - b + owner) if d % 2 == b else None
            )
        swapped_upper[j] = routed(
            uppers[j], lambda t, d, owner=owner: (t, d + 2 * owner - 1) if d % 2 == 1 - owner else None
        )
    gradient = []
    for layer in range(layers):
        first, second = layer, layers + layer
        kept = jnp.where(member == 0, uppers[first], uppers[second])
        given = swapped_upper[first] + swapped_upper[second]
        grad = place_columns(kept, my_column, width) + place_columns(given, other_column, width)
        for b in range(2):
            grad = grad + place_columns(lowers[first][b] + lowers[second][b], before[b, 1], width)
        gradient.append(grad)
    return jnp.stack(gradient, axis=0)


def solution(mesh):
    return jax.shard_map(
        body,
        mesh=mesh,
        in_specs=(
            P(),
            P("depth", None, ("groups", "scan"), None),
            P(("groups", "scan"), None),
            P(("groups", "scan")),
            P(("groups", "scan"), None, None),
        ),
        out_specs=P("depth", None, ("groups", "scan"), None),
        check_vma=False,
    )
```

```python
import math

import jax
import numpy as np
import jax.numpy as jnp
from jax import lax
from jax.sharding import PartitionSpec as P

chirp_rate = 0.25


def shifted(block, axis, distance):
    devices = range(lax.axis_size(axis))
    route = [((i - distance) % len(devices), i) for i in devices]
    return lax.ppermute(block, axis, route)


def passed_along(block, axis, distance):
    devices = range(lax.axis_size(axis))
    route = [(i - distance, i) for i in devices if i - distance in devices]
    return lax.ppermute(block, axis, route)


def make_tables(length):
    index = np.arange(length)
    product = index[:, None] * index[None, :] % length
    angle = 2.0 * math.pi / length * product
    factor = 1.0 / math.sqrt(length)
    freq = np.where(index < length // 2, index, index - length).astype(np.float64)
    theta = -math.pi * chirp_rate / length * (freq[:, None] ** 2 + freq[None, :] ** 2)
    values = (np.cos(angle) * factor, -np.sin(angle) * factor, np.cos(theta), np.sin(theta))
    return tuple(jnp.asarray(value.astype(np.float32)) for value in values)


def left_product(matrix, field):
    return jnp.einsum(
        "jk,...kl->...jl",
        matrix,
        field,
        preferred_element_type=jnp.float32,
        precision=lax.Precision.HIGHEST,
    )


def right_product(field, matrix):
    return jnp.einsum(
        "...jk,kl->...jl",
        field,
        matrix,
        preferred_element_type=jnp.float32,
        precision=lax.Precision.HIGHEST,
    )


def transform(field, tables, forward):
    table_real = tables[0]
    table_imag = tables[1] if forward else -tables[1]
    real_part = field[..., 0, :, :]
    imag_part = field[..., 1, :, :]
    first_real = left_product(table_real, real_part) - left_product(table_imag, imag_part)
    first_imag = left_product(table_real, imag_part) + left_product(table_imag, real_part)
    out_real = right_product(first_real, table_real) - right_product(first_imag, table_imag)
    out_imag = right_product(first_real, table_imag) + right_product(first_imag, table_real)
    return jnp.stack([out_real, out_imag], axis=-3)


def complex_product(first, second, conjugate):
    first_real = first[..., 0, :, :]
    first_imag = first[..., 1, :, :]
    if conjugate:
        first_imag = -first_imag
    second_real = second[..., 0, :, :]
    second_imag = second[..., 1, :, :]
    return jnp.stack(
        [
            first_real * second_real - first_imag * second_imag,
            first_real * second_imag + first_imag * second_real,
        ],
        axis=-3,
    )


def propagate(field, tables, forward):
    spectrum = transform(field, tables, True)
    sine = tables[3] if forward else -tables[3]
    chirp = jnp.stack([tables[2], sine], axis=0)
    return transform(complex_product(spectrum, chirp, False), tables, False)


def far_field(exit_wave, measured, live, tables):
    spectrum = transform(exit_wave, tables, True)
    power = spectrum[..., 0, :, :] ** 2 + spectrum[..., 1, :, :] ** 2
    keep = live[:, None, None] * (1.0 - measured / jnp.sqrt(power + 1.0))
    residual = spectrum * keep[..., None, :, :]
    return transform(residual, tables, False)


def cut_columns(block, column, width):
    zero = jnp.zeros((), jnp.int32)
    start = (zero,) * (block.ndim - 1) + (column,)
    return lax.dynamic_slice(block, start, block.shape[:-1] + (width,))


def cut_rows(block, row, height):
    zero = jnp.zeros((), jnp.int32)
    start = (zero,) * (block.ndim - 2) + (row, zero)
    return lax.dynamic_slice(block, start, block.shape[:-2] + (height, block.shape[-1]))


def place_columns(block, column, width):
    pad = [(0, 0)] * (block.ndim - 1) + [(width, width - block.shape[-1])]
    return cut_columns(jnp.pad(block, pad), width - column, width)


def pick(stack, index):
    return lax.dynamic_index_in_dim(stack, index, 0, keepdims=False)


def swapped(block, axis):
    return lax.ppermute(block, axis, [(i, i ^ 1) for i in range(lax.axis_size(axis))])


def routed(block, destination):
    tiles = lax.axis_size("scan")
    groups = lax.axis_size("depth")
    route = []
    for t in range(tiles):
        for d in range(groups):
            target = destination(t, d)
            if target is not None:
                route.append((t * groups + d, (target[0] % tiles) * groups + target[1]))
    return lax.ppermute(block, ("scan", "depth"), route)


def body(probe, slices, positions, counts, amplitude):
    patch = probe.shape[-1]
    slots = positions.shape[0]
    layers = slices.shape[0]
    tile_rows = slices.shape[2]
    width = slices.shape[3]
    tables = lax.optimization_barrier(make_tables(patch))
    depth_index = lax.axis_index("depth")
    depth_count = lax.axis_size("depth")
    assert slots == 2 and depth_count % 2 == 0
    pairs = depth_count // 2
    pair = depth_index // 2
    member = depth_index % 2
    span = 2 * layers
    before = shifted(positions, "scan", 1)
    own_rows = slices[:, :, :patch]
    my_row = jnp.where(member == 0, positions[0, 0], positions[1, 0])
    my_column = jnp.where(member == 0, positions[0, 1], positions[1, 1])
    other_column = jnp.where(member == 0, positions[1, 1], positions[0, 1])

    swapped_rows = [swapped(cut_columns(own_rows[layer], other_column, patch), "depth") for layer in range(layers)]
    below = [None] * span
    previous = None
    for source in range(2):
        for layer in range(layers):
            got = []
            for b in range(slots):
                piece = cut_columns(own_rows[layer], before[b, 1], patch)
                if previous is None:
                    probe, piece = lax.optimization_barrier((probe, piece))
                else:
                    piece, previous = lax.optimization_barrier((piece, previous))
                got.append(
                    routed(
                        piece,
                        lambda t, d, b=b, source=source: (t - 1, d - source + b) if d % 2 == source else None,
                    )
                )
            previous = got[0] + got[1]
            below[source * layers + layer] = previous
    path = []
    for j in range(span):
        source = j // layers
        own = cut_columns(own_rows[j % layers], my_column, patch)
        own = jnp.where(member == source, own, swapped_rows[j % layers])
        path.append(cut_rows(jnp.concatenate([own, below[j]], axis=-2), my_row, patch))
    live = (jnp.arange(slots, dtype=jnp.int32) < counts[0]).astype(jnp.float32)
    my_live = jnp.where(member == 0, live[0], live[1])[None]
    my_amplitude = jnp.where(member == 0, amplitude[0], amplitude[1])[None]

    first_psi = propagate(probe[None], tables, True)[0]
    wave_now = None
    saved = []
    for step_number in range(pairs):
        psis = []
        for j in range(span):
            if j == 0 and step_number == 0:
                psi = first_psi
            else:
                psi = propagate(wave_now, tables, True)
            psis.append(psi)
            wave_now = complex_product(psi, path[j], False)
        saved.append(psis)
        if step_number < pairs - 1:
            wave_now = passed_along(wave_now, "depth", 2)
    chi_wave = far_field(wave_now[None], my_amplitude, my_live, tables)[0]

    blank = jnp.zeros((2, patch, patch), jnp.float32)
    uppers = [None] * span
    lowers = [[None] * 2 for _ in range(span)]
    swapped_upper = [None] * span

    def send_terms(j):
        if pairs == 1:
            mine = terms[0][j]
        else:
            mine = pick(jnp.stack([terms[k][j] for k in range(pairs)], axis=0), pair)
        padded = jnp.concatenate([blank, mine, blank], axis=-2)
        uppers[j] = cut_rows(padded, patch - my_row, patch)
        lower = cut_rows(padded, 2 * patch - my_row, patch)
        owner = j // layers
        for b in range(2):
            lowers[j][b] = routed(
                lower, lambda t, d, b=b, owner=owner: (t + 1, d - b + owner) if d % 2 == b else None
            )
        swapped_upper[j] = routed(
            uppers[j], lambda t, d, owner=owner: (t, d + 2 * owner - 1) if d % 2 == 1 - owner else None
        )

    terms = [[None] * span for _ in range(pairs)]
    for step_number in range(pairs - 1, -1, -1):
        for j in range(span - 1, -1, -1):
            terms[step_number][j] = complex_product(saved[step_number][j], chi_wave, True)
            if step_number == 0:
                send_terms(j)
            if j == 0 and step_number == 0:
                continue
            back = complex_product(path[j], chi_wave, True)
            if step_number == 0 and j + 2 < span:
                done = (lowers[j + 2][0], lowers[j + 2][1], swapped_upper[j + 2])
                back, done = lax.optimization_barrier((back, done))
                lowers[j + 2][0], lowers[j + 2][1], swapped_upper[j + 2] = done
            chi_wave = propagate(back, tables, False)
        if step_number > 0:
            chi_wave = passed_along(chi_wave, "depth", -2)

    gradient = []
    for layer in range(layers):
        first, second = layer, layers + layer
        kept = jnp.where(member == 0, uppers[first], uppers[second])
        given = swapped_upper[first] + swapped_upper[second]
        grad = place_columns(kept, my_column, width) + place_columns(given, other_column, width)
        for b in range(2):
            grad = grad + place_columns(lowers[first][b] + lowers[second][b], before[b, 1], width)
        gradient.append(grad)
    return jnp.stack(gradient, axis=0)


def solution(mesh):
    return jax.shard_map(
        body,
        mesh=mesh,
        in_specs=(
            P(),
            P("depth", None, ("groups", "scan"), None),
            P(("groups", "scan"), None),
            P(("groups", "scan")),
            P(("groups", "scan"), None, None),
        ),
        out_specs=P("depth", None, ("groups", "scan"), None),
        check_vma=False,
    )
```

```python
import math

import jax
import numpy as np
import jax.numpy as jnp
from jax import lax
from jax.sharding import PartitionSpec as P

chirp_rate = 0.25


def shifted(block, axis, distance):
    devices = range(lax.axis_size(axis))
    route = [((i - distance) % len(devices), i) for i in devices]
    return lax.ppermute(block, axis, route)


def passed_along(block, axis, distance):
    devices = range(lax.axis_size(axis))
    route = [(i - distance, i) for i in devices if i - distance in devices]
    return lax.ppermute(block, axis, route)


def make_tables(length):
    index = np.arange(length)
    product = index[:, None] * index[None, :] % length
    angle = 2.0 * math.pi / length * product
    factor = 1.0 / math.sqrt(length)
    freq = np.where(index < length // 2, index, index - length).astype(np.float64)
    theta = -math.pi * chirp_rate / length * (freq[:, None] ** 2 + freq[None, :] ** 2)
    values = (np.cos(angle) * factor, -np.sin(angle) * factor, np.cos(theta), np.sin(theta))
    return tuple(jnp.asarray(value.astype(np.float32)) for value in values)


def left_product(matrix, field):
    return jnp.einsum(
        "jk,...kl->...jl",
        matrix,
        field,
        preferred_element_type=jnp.float32,
        precision=lax.Precision.HIGHEST,
    )


def right_product(field, matrix):
    return jnp.einsum(
        "...jk,kl->...jl",
        field,
        matrix,
        preferred_element_type=jnp.float32,
        precision=lax.Precision.HIGHEST,
    )


def transform(field, tables, forward):
    table_real = tables[0]
    table_imag = tables[1] if forward else -tables[1]
    real_part = field[..., 0, :, :]
    imag_part = field[..., 1, :, :]
    first_real = left_product(table_real, real_part) - left_product(table_imag, imag_part)
    first_imag = left_product(table_real, imag_part) + left_product(table_imag, real_part)
    out_real = right_product(first_real, table_real) - right_product(first_imag, table_imag)
    out_imag = right_product(first_real, table_imag) + right_product(first_imag, table_real)
    return jnp.stack([out_real, out_imag], axis=-3)


def complex_product(first, second, conjugate):
    first_real = first[..., 0, :, :]
    first_imag = first[..., 1, :, :]
    if conjugate:
        first_imag = -first_imag
    second_real = second[..., 0, :, :]
    second_imag = second[..., 1, :, :]
    return jnp.stack(
        [
            first_real * second_real - first_imag * second_imag,
            first_real * second_imag + first_imag * second_real,
        ],
        axis=-3,
    )


def propagate(field, tables, forward):
    spectrum = transform(field, tables, True)
    sine = tables[3] if forward else -tables[3]
    chirp = jnp.stack([tables[2], sine], axis=0)
    return transform(complex_product(spectrum, chirp, False), tables, False)


def far_field(exit_wave, measured, live, tables):
    spectrum = transform(exit_wave, tables, True)
    power = spectrum[..., 0, :, :] ** 2 + spectrum[..., 1, :, :] ** 2
    keep = live[:, None, None] * (1.0 - measured / jnp.sqrt(power + 1.0))
    residual = spectrum * keep[..., None, :, :]
    return transform(residual, tables, False)


def cut_columns(block, column, width):
    zero = jnp.zeros((), jnp.int32)
    start = (zero,) * (block.ndim - 1) + (column,)
    return lax.dynamic_slice(block, start, block.shape[:-1] + (width,))


def cut_rows(block, row, height):
    zero = jnp.zeros((), jnp.int32)
    start = (zero,) * (block.ndim - 2) + (row, zero)
    return lax.dynamic_slice(block, start, block.shape[:-2] + (height, block.shape[-1]))


def place_columns(block, column, width):
    pad = [(0, 0)] * (block.ndim - 1) + [(width, width - block.shape[-1])]
    return cut_columns(jnp.pad(block, pad), width - column, width)


def pick(stack, index):
    return lax.dynamic_index_in_dim(stack, index, 0, keepdims=False)


def swapped(block, axis):
    return lax.ppermute(block, axis, [(i, i ^ 1) for i in range(lax.axis_size(axis))])


def routed(block, destination):
    tiles = lax.axis_size("scan")
    groups = lax.axis_size("depth")
    route = []
    for t in range(tiles):
        for d in range(groups):
            target = destination(t, d)
            if target is not None:
                route.append((t * groups + d, (target[0] % tiles) * groups + target[1]))
    return lax.ppermute(block, ("scan", "depth"), route)


def body(probe, slices, positions, counts, amplitude):
    patch = probe.shape[-1]
    slots = positions.shape[0]
    layers = slices.shape[0]
    tile_rows = slices.shape[2]
    width = slices.shape[3]
    tables = lax.optimization_barrier(make_tables(patch))
    depth_index = lax.axis_index("depth")
    depth_count = lax.axis_size("depth")
    assert slots == 2 and depth_count % 2 == 0
    pairs = depth_count // 2
    pair = depth_index // 2
    member = depth_index % 2
    span = 2 * layers
    before = shifted(positions, "scan", 1)
    own_rows = slices[:, :, :patch]
    my_row = jnp.where(member == 0, positions[0, 0], positions[1, 0])
    my_column = jnp.where(member == 0, positions[0, 1], positions[1, 1])
    other_column = jnp.where(member == 0, positions[1, 1], positions[0, 1])

    swapped_rows = [swapped(cut_columns(own_rows[layer], other_column, patch), "depth") for layer in range(layers)]
    below = [None] * span
    previous = None
    for source in range(2):
        for layer in range(layers):
            got = []
            for b in range(slots):
                piece = cut_columns(own_rows[layer], before[b, 1], patch)
                if previous is None:
                    probe, piece = lax.optimization_barrier((probe, piece))
                else:
                    piece, previous = lax.optimization_barrier((piece, previous))
                got.append(
                    routed(
                        piece,
                        lambda t, d, b=b, source=source: (t - 1, d - source + b) if d % 2 == source else None,
                    )
                )
            previous = got[0] + got[1]
            below[source * layers + layer] = previous
    path = []
    for j in range(span):
        source = j // layers
        own = cut_columns(own_rows[j % layers], my_column, patch)
        own = jnp.where(member == source, own, swapped_rows[j % layers])
        path.append(cut_rows(jnp.concatenate([own, below[j]], axis=-2), my_row, patch))
    live = (jnp.arange(slots, dtype=jnp.int32) < counts[0]).astype(jnp.float32)
    my_live = jnp.where(member == 0, live[0], live[1])[None]
    my_amplitude = jnp.where(member == 0, amplitude[0], amplitude[1])[None]

    first_psi = propagate(probe[None], tables, True)[0]
    wave_now = None
    saved = []
    for step_number in range(pairs):
        psis = []
        for j in range(span):
            if j == 0 and step_number == 0:
                psi = first_psi
            else:
                psi = propagate(wave_now, tables, True)
            psis.append(psi)
            wave_now = complex_product(psi, path[j], False)
        saved.append(psis)
        if step_number < pairs - 1:
            wave_now = passed_along(wave_now, "depth", 2)
    chi_wave = far_field(wave_now[None], my_amplitude, my_live, tables)[0]

    blank = jnp.zeros((2, patch, patch), jnp.float32)
    uppers = [None] * span
    lowers = [[None] * 2 for _ in range(span)]
    swapped_upper = [None] * span

    def send_terms(j):
        if pairs == 1:
            mine = terms[0][j]
        else:
            mine = pick(jnp.stack([terms[k][j] for k in range(pairs)], axis=0), pair)
        padded = jnp.concatenate([blank, mine, blank], axis=-2)
        uppers[j] = cut_rows(padded, patch - my_row, patch)
        lower = cut_rows(padded, 2 * patch - my_row, patch)
        owner = j // layers
        for b in range(2):
            lowers[j][b] = routed(
                lower, lambda t, d, b=b, owner=owner: (t + 1, d - b + owner) if d % 2 == b else None
            )
        swapped_upper[j] = routed(
            uppers[j], lambda t, d, owner=owner: (t, d + 2 * owner - 1) if d % 2 == 1 - owner else None
        )

    terms = [[None] * span for _ in range(pairs)]
    for step_number in range(pairs - 1, -1, -1):
        for j in range(span - 1, -1, -1):
            terms[step_number][j] = complex_product(saved[step_number][j], chi_wave, True)
            if step_number == 0:
                send_terms(j)
            if j == 0 and step_number == 0:
                continue
            back = complex_product(path[j], chi_wave, True)
            chi_wave = propagate(back, tables, False)
        if step_number > 0:
            chi_wave = passed_along(chi_wave, "depth", -2)

    gradient = []
    for layer in range(layers):
        first, second = layer, layers + layer
        kept = jnp.where(member == 0, uppers[first], uppers[second])
        given = swapped_upper[first] + swapped_upper[second]
        grad = place_columns(kept, my_column, width) + place_columns(given, other_column, width)
        for b in range(2):
            grad = grad + place_columns(lowers[first][b] + lowers[second][b], before[b, 1], width)
        gradient.append(grad)
    return jnp.stack(gradient, axis=0)


def solution(mesh):
    return jax.shard_map(
        body,
        mesh=mesh,
        in_specs=(
            P(),
            P("depth", None, ("groups", "scan"), None),
            P(("groups", "scan"), None),
            P(("groups", "scan")),
            P(("groups", "scan"), None, None),
        ),
        out_specs=P("depth", None, ("groups", "scan"), None),
        check_vma=False,
    )
```

```python
import math

import jax
import jax.numpy as jnp
from jax import lax
from jax.sharding import PartitionSpec as P

chirp_rate = 0.25


def shifted(block, axis, distance):
    devices = range(lax.axis_size(axis))
    route = [((i - distance) % len(devices), i) for i in devices]
    return lax.ppermute(block, axis, route)


def passed_along(block, axis, distance):
    devices = range(lax.axis_size(axis))
    route = [(i - distance, i) for i in devices if i - distance in devices]
    return lax.ppermute(block, axis, route)


def make_tables(length):
    index = jnp.arange(length, dtype=jnp.int32)
    product = index[:, None] * index[None, :] % length
    angle = 2.0 * math.pi / length * product.astype(jnp.float32)
    factor = 1.0 / math.sqrt(length)
    table_real = jnp.cos(angle) * factor
    table_imag = -jnp.sin(angle) * factor
    freq = jnp.where(index < length // 2, index, index - length).astype(jnp.float32)
    theta = -math.pi * chirp_rate / length * (freq[:, None] ** 2 + freq[None, :] ** 2)
    return (table_real, table_imag, jnp.cos(theta), jnp.sin(theta))


def left_product(matrix, field):
    return jnp.einsum(
        "jk,...kl->...jl",
        matrix,
        field,
        preferred_element_type=jnp.float32,
        precision=lax.Precision.HIGHEST,
    )


def right_product(field, matrix):
    return jnp.einsum(
        "...jk,kl->...jl",
        field,
        matrix,
        preferred_element_type=jnp.float32,
        precision=lax.Precision.HIGHEST,
    )


def transform(field, tables, forward):
    table_real = tables[0]
    table_imag = tables[1] if forward else -tables[1]
    real_part = field[..., 0, :, :]
    imag_part = field[..., 1, :, :]
    first_real = left_product(table_real, real_part) - left_product(table_imag, imag_part)
    first_imag = left_product(table_real, imag_part) + left_product(table_imag, real_part)
    out_real = right_product(first_real, table_real) - right_product(first_imag, table_imag)
    out_imag = right_product(first_real, table_imag) + right_product(first_imag, table_real)
    return jnp.stack([out_real, out_imag], axis=-3)


def complex_product(first, second, conjugate):
    first_real = first[..., 0, :, :]
    first_imag = first[..., 1, :, :]
    if conjugate:
        first_imag = -first_imag
    second_real = second[..., 0, :, :]
    second_imag = second[..., 1, :, :]
    return jnp.stack(
        [
            first_real * second_real - first_imag * second_imag,
            first_real * second_imag + first_imag * second_real,
        ],
        axis=-3,
    )


def propagate(field, tables, forward):
    spectrum = transform(field, tables, True)
    sine = tables[3] if forward else -tables[3]
    chirp = jnp.stack([tables[2], sine], axis=0)
    return transform(complex_product(spectrum, chirp, False), tables, False)


def far_field(exit_wave, measured, live, tables):
    spectrum = transform(exit_wave, tables, True)
    power = spectrum[..., 0, :, :] ** 2 + spectrum[..., 1, :, :] ** 2
    keep = live[:, None, None] * (1.0 - measured / jnp.sqrt(power + 1.0))
    residual = spectrum * keep[..., None, :, :]
    return transform(residual, tables, False)


def cut_columns(block, column, width):
    zero = jnp.zeros((), jnp.int32)
    start = (zero,) * (block.ndim - 1) + (column,)
    return lax.dynamic_slice(block, start, block.shape[:-1] + (width,))


def cut_rows(block, row, height):
    zero = jnp.zeros((), jnp.int32)
    start = (zero,) * (block.ndim - 2) + (row, zero)
    return lax.dynamic_slice(block, start, block.shape[:-2] + (height, block.shape[-1]))


def place_columns(block, column, width):
    pad = [(0, 0)] * (block.ndim - 1) + [(width, width - block.shape[-1])]
    return cut_columns(jnp.pad(block, pad), width - column, width)


def pick(stack, index):
    return lax.dynamic_index_in_dim(stack, index, 0, keepdims=False)


def swapped(block, axis):
    return lax.ppermute(block, axis, [(i, i ^ 1) for i in range(lax.axis_size(axis))])


def routed(block, destination):
    tiles = lax.axis_size("scan")
    groups = lax.axis_size("depth")
    route = []
    for t in range(tiles):
        for d in range(groups):
            target = destination(t, d)
            if target is not None:
                route.append((t * groups + d, (target[0] % tiles) * groups + target[1]))
    return lax.ppermute(block, ("scan", "depth"), route)


def body(probe, slices, positions, counts, amplitude):
    patch = probe.shape[-1]
    slots = positions.shape[0]
    layers = slices.shape[0]
    tile_rows = slices.shape[2]
    width = slices.shape[3]
    tables = lax.optimization_barrier(make_tables(patch))
    depth_index = lax.axis_index("depth")
    depth_count = lax.axis_size("depth")
    assert slots == 2 and depth_count % 2 == 0
    pairs = depth_count // 2
    pair = depth_index // 2
    member = depth_index % 2
    span = 2 * layers
    before = shifted(positions, "scan", 1)
    own_rows = slices[:, :, :patch]
    my_row = jnp.where(member == 0, positions[0, 0], positions[1, 0])
    my_column = jnp.where(member == 0, positions[0, 1], positions[1, 1])
    other_column = jnp.where(member == 0, positions[1, 1], positions[0, 1])

    swapped_rows = [swapped(cut_columns(own_rows[layer], other_column, patch), "depth") for layer in range(layers)]
    below = [None] * span
    previous = None
    for source in range(2):
        for layer in range(layers):
            got = []
            for b in range(slots):
                piece = cut_columns(own_rows[layer], before[b, 1], patch)
                if previous is None:
                    probe, piece = lax.optimization_barrier((probe, piece))
                else:
                    piece, previous = lax.optimization_barrier((piece, previous))
                got.append(
                    routed(
                        piece,
                        lambda t, d, b=b, source=source: (t - 1, d - source + b) if d % 2 == source else None,
                    )
                )
            previous = got[0] + got[1]
            below[source * layers + layer] = previous
    path = []
    for j in range(span):
        source = j // layers
        own = cut_columns(own_rows[j % layers], my_column, patch)
        own = jnp.where(member == source, own, swapped_rows[j % layers])
        path.append(cut_rows(jnp.concatenate([own, below[j]], axis=-2), my_row, patch))
    live = (jnp.arange(slots, dtype=jnp.int32) < counts[0]).astype(jnp.float32)
    my_live = jnp.where(member == 0, live[0], live[1])[None]
    my_amplitude = jnp.where(member == 0, amplitude[0], amplitude[1])[None]

    first_psi = propagate(probe[None], tables, True)[0]
    wave_now = None
    saved = []
    for step_number in range(pairs):
        psis = []
        for j in range(span):
            if j == 0 and step_number == 0:
                psi = first_psi
            else:
                psi = propagate(wave_now, tables, True)
            psis.append(psi)
            wave_now = complex_product(psi, path[j], False)
        saved.append(psis)
        if step_number < pairs - 1:
            wave_now = passed_along(wave_now, "depth", 2)
    chi_wave = far_field(wave_now[None], my_amplitude, my_live, tables)[0]

    terms = [None] * pairs
    for step_number in range(pairs - 1, -1, -1):
        found = [None] * span
        for j in range(span - 1, -1, -1):
            found[j] = complex_product(saved[step_number][j], chi_wave, True)
            if j == 0 and step_number == 0:
                continue
            back = complex_product(path[j], chi_wave, True)
            chi_wave = propagate(back, tables, False)
        terms[step_number] = found
        if step_number > 0:
            chi_wave = passed_along(chi_wave, "depth", -2)

    blank = jnp.zeros((2, patch, patch), jnp.float32)
    uppers = [None] * span
    lowers = [None] * span
    for j in range(span - 1, -1, -1):
        if pairs == 1:
            mine = terms[0][j]
        else:
            mine = pick(jnp.stack([terms[k][j] for k in range(pairs)], axis=0), pair)
        padded = jnp.concatenate([blank, mine, blank], axis=-2)
        uppers[j] = cut_rows(padded, patch - my_row, patch)
        lowers[j] = cut_rows(padded, 2 * patch - my_row, patch)
    arrived = [[None] * 2 for _ in range(2)]
    given = [None] * 2
    for owner in (1, 0):
        group_lower = jnp.stack(lowers[owner * layers : (owner + 1) * layers], axis=0)
        group_upper = jnp.stack(uppers[owner * layers : (owner + 1) * layers], axis=0)
        for b in range(2):
            arrived[owner][b] = routed(
                group_lower, lambda t, d, b=b, owner=owner: (t + 1, d - b + owner) if d % 2 == b else None
            )
        given[owner] = routed(
            group_upper, lambda t, d, owner=owner: (t, d + 2 * owner - 1) if d % 2 == 1 - owner else None
        )
    gradient = []
    for layer in range(layers):
        first, second = layer, layers + layer
        kept = jnp.where(member == 0, uppers[first], uppers[second])
        grad = place_columns(kept, my_column, width)
        grad = grad + place_columns(given[0][layer] + given[1][layer], other_column, width)
        for b in range(2):
            grad = grad + place_columns(arrived[0][b][layer] + arrived[1][b][layer], before[b, 1], width)
        gradient.append(grad)
    return jnp.stack(gradient, axis=0)


def solution(mesh):
    return jax.shard_map(
        body,
        mesh=mesh,
        in_specs=(
            P(),
            P("depth", None, ("groups", "scan"), None),
            P(("groups", "scan"), None),
            P(("groups", "scan")),
            P(("groups", "scan"), None, None),
        ),
        out_specs=P("depth", None, ("groups", "scan"), None),
        check_vma=False,
    )
```

```python
import math

import jax
import jax.numpy as jnp
from jax import lax
from jax.sharding import PartitionSpec as P

chirp_rate = 0.25


def shifted(block, axis, distance):
    devices = range(lax.axis_size(axis))
    route = [((i - distance) % len(devices), i) for i in devices]
    return lax.ppermute(block, axis, route)


def passed_along(block, axis, distance):
    devices = range(lax.axis_size(axis))
    route = [(i - distance, i) for i in devices if i - distance in devices]
    return lax.ppermute(block, axis, route)


def make_tables(length):
    index = jnp.arange(length, dtype=jnp.int32)
    product = index[:, None] * index[None, :] % length
    angle = 2.0 * math.pi / length * product.astype(jnp.float32)
    factor = 1.0 / math.sqrt(length)
    table_real = jnp.cos(angle) * factor
    table_imag = -jnp.sin(angle) * factor
    freq = jnp.where(index < length // 2, index, index - length).astype(jnp.float32)
    theta = -math.pi * chirp_rate / length * (freq[:, None] ** 2 + freq[None, :] ** 2)
    return (table_real, table_imag, jnp.cos(theta), jnp.sin(theta))


def left_product(matrix, field):
    return jnp.einsum(
        "jk,...kl->...jl",
        matrix,
        field,
        preferred_element_type=jnp.float32,
        precision=lax.Precision.HIGHEST,
    )


def right_product(field, matrix):
    return jnp.einsum(
        "...jk,kl->...jl",
        field,
        matrix,
        preferred_element_type=jnp.float32,
        precision=lax.Precision.HIGHEST,
    )


def transform(field, tables, forward):
    table_real = tables[0]
    table_imag = tables[1] if forward else -tables[1]
    real_part = field[..., 0, :, :]
    imag_part = field[..., 1, :, :]
    first_real = left_product(table_real, real_part) - left_product(table_imag, imag_part)
    first_imag = left_product(table_real, imag_part) + left_product(table_imag, real_part)
    out_real = right_product(first_real, table_real) - right_product(first_imag, table_imag)
    out_imag = right_product(first_real, table_imag) + right_product(first_imag, table_real)
    return jnp.stack([out_real, out_imag], axis=-3)


def complex_product(first, second, conjugate):
    first_real = first[..., 0, :, :]
    first_imag = first[..., 1, :, :]
    if conjugate:
        first_imag = -first_imag
    second_real = second[..., 0, :, :]
    second_imag = second[..., 1, :, :]
    return jnp.stack(
        [
            first_real * second_real - first_imag * second_imag,
            first_real * second_imag + first_imag * second_real,
        ],
        axis=-3,
    )


def propagate(field, tables, forward):
    spectrum = transform(field, tables, True)
    sine = tables[3] if forward else -tables[3]
    chirp = jnp.stack([tables[2], sine], axis=0)
    return transform(complex_product(spectrum, chirp, False), tables, False)


def far_field(exit_wave, measured, live, tables):
    spectrum = transform(exit_wave, tables, True)
    power = spectrum[..., 0, :, :] ** 2 + spectrum[..., 1, :, :] ** 2
    keep = live[:, None, None] * (1.0 - measured / jnp.sqrt(power + 1.0))
    residual = spectrum * keep[..., None, :, :]
    return transform(residual, tables, False)


def cut_columns(block, column, width):
    zero = jnp.zeros((), jnp.int32)
    start = (zero,) * (block.ndim - 1) + (column,)
    return lax.dynamic_slice(block, start, block.shape[:-1] + (width,))


def cut_rows(block, row, height):
    zero = jnp.zeros((), jnp.int32)
    start = (zero,) * (block.ndim - 2) + (row, zero)
    return lax.dynamic_slice(block, start, block.shape[:-2] + (height, block.shape[-1]))


def place_columns(block, column, width):
    pad = [(0, 0)] * (block.ndim - 1) + [(width, width - block.shape[-1])]
    return cut_columns(jnp.pad(block, pad), width - column, width)


def pick(stack, index):
    return lax.dynamic_index_in_dim(stack, index, 0, keepdims=False)


def swapped(block, axis):
    return lax.ppermute(block, axis, [(i, i ^ 1) for i in range(lax.axis_size(axis))])


def routed(block, destination):
    tiles = lax.axis_size("scan")
    groups = lax.axis_size("depth")
    route = []
    for t in range(tiles):
        for d in range(groups):
            target = destination(t, d)
            if target is not None:
                route.append((t * groups + d, (target[0] % tiles) * groups + target[1]))
    return lax.ppermute(block, ("scan", "depth"), route)


def body(probe, slices, positions, counts, amplitude):
    patch = probe.shape[-1]
    slots = positions.shape[0]
    layers = slices.shape[0]
    tile_rows = slices.shape[2]
    width = slices.shape[3]
    tables = lax.optimization_barrier(make_tables(patch))
    depth_index = lax.axis_index("depth")
    depth_count = lax.axis_size("depth")
    assert slots == 2 and depth_count % 2 == 0
    pairs = depth_count // 2
    pair = depth_index // 2
    member = depth_index % 2
    span = 2 * layers
    before = shifted(positions, "scan", 1)
    own_rows = slices[:, :, :patch]
    my_row = jnp.where(member == 0, positions[0, 0], positions[1, 0])
    my_column = jnp.where(member == 0, positions[0, 1], positions[1, 1])
    other_column = jnp.where(member == 0, positions[1, 1], positions[0, 1])

    swapped_rows = [swapped(cut_columns(own_rows[layer], other_column, patch), "depth") for layer in range(layers)]
    below = [None] * span
    previous = None
    for source in range(2):
        for layer in range(layers):
            got = []
            for b in range(slots):
                piece = cut_columns(own_rows[layer], before[b, 1], patch)
                if previous is not None:
                    piece, previous = lax.optimization_barrier((piece, previous))
                got.append(
                    routed(
                        piece,
                        lambda t, d, b=b, source=source: (t - 1, d - source + b) if d % 2 == source else None,
                    )
                )
            previous = got[0] + got[1]
            if source == 0 and layer == 0:
                probe, previous = lax.optimization_barrier((probe, previous))
            below[source * layers + layer] = previous
    path = []
    for j in range(span):
        source = j // layers
        own = cut_columns(own_rows[j % layers], my_column, patch)
        own = jnp.where(member == source, own, swapped_rows[j % layers])
        path.append(cut_rows(jnp.concatenate([own, below[j]], axis=-2), my_row, patch))
    live = (jnp.arange(slots, dtype=jnp.int32) < counts[0]).astype(jnp.float32)
    my_live = jnp.where(member == 0, live[0], live[1])[None]
    my_amplitude = jnp.where(member == 0, amplitude[0], amplitude[1])[None]

    first_psi = propagate(probe[None], tables, True)[0]
    wave_now = None
    saved = []
    for step_number in range(pairs):
        psis = []
        for j in range(span):
            if j == 0 and step_number == 0:
                psi = first_psi
            else:
                psi = propagate(wave_now, tables, True)
            psis.append(psi)
            wave_now = complex_product(psi, path[j], False)
        saved.append(psis)
        if step_number < pairs - 1:
            wave_now = passed_along(wave_now, "depth", 2)
    chi_wave = far_field(wave_now[None], my_amplitude, my_live, tables)[0]

    terms = [None] * pairs
    for step_number in range(pairs - 1, -1, -1):
        found = [None] * span
        for j in range(span - 1, -1, -1):
            found[j] = complex_product(saved[step_number][j], chi_wave, True)
            if j == 0 and step_number == 0:
                continue
            back = complex_product(path[j], chi_wave, True)
            chi_wave = propagate(back, tables, False)
        terms[step_number] = found
        if step_number > 0:
            chi_wave = passed_along(chi_wave, "depth", -2)

    blank = jnp.zeros((2, patch, patch), jnp.float32)
    uppers = [None] * span
    lowers = [[None] * 2 for _ in range(span)]
    swapped_upper = [None] * span
    for j in range(span - 1, -1, -1):
        if pairs == 1:
            mine = terms[0][j]
        else:
            mine = pick(jnp.stack([terms[k][j] for k in range(pairs)], axis=0), pair)
        padded = jnp.concatenate([blank, mine, blank], axis=-2)
        uppers[j] = cut_rows(padded, patch - my_row, patch)
        lower = cut_rows(padded, 2 * patch - my_row, patch)
        owner = j // layers
        for b in range(2):
            lowers[j][b] = routed(
                lower, lambda t, d, b=b, owner=owner: (t + 1, d - b + owner) if d % 2 == b else None
            )
        swapped_upper[j] = routed(
            uppers[j], lambda t, d, owner=owner: (t, d + 2 * owner - 1) if d % 2 == 1 - owner else None
        )
    gradient = []
    for layer in range(layers):
        first, second = layer, layers + layer
        kept = jnp.where(member == 0, uppers[first], uppers[second])
        given = swapped_upper[first] + swapped_upper[second]
        grad = place_columns(kept, my_column, width) + place_columns(given, other_column, width)
        for b in range(2):
            grad = grad + place_columns(lowers[first][b] + lowers[second][b], before[b, 1], width)
        gradient.append(grad)
    return jnp.stack(gradient, axis=0)


def solution(mesh):
    return jax.shard_map(
        body,
        mesh=mesh,
        in_specs=(
            P(),
            P("depth", None, ("groups", "scan"), None),
            P(("groups", "scan"), None),
            P(("groups", "scan")),
            P(("groups", "scan"), None, None),
        ),
        out_specs=P("depth", None, ("groups", "scan"), None),
        check_vma=False,
    )
```

```python
import math

import jax
import jax.numpy as jnp
from jax import lax
from jax.sharding import PartitionSpec as P

chirp_rate = 0.25


def shifted(block, axis, distance):
    devices = range(lax.axis_size(axis))
    route = [((i - distance) % len(devices), i) for i in devices]
    return lax.ppermute(block, axis, route)


def passed_along(block, axis, distance):
    devices = range(lax.axis_size(axis))
    route = [(i - distance, i) for i in devices if i - distance in devices]
    return lax.ppermute(block, axis, route)


def make_tables(length):
    index = jnp.arange(length, dtype=jnp.int32)
    product = index[:, None] * index[None, :] % length
    angle = 2.0 * math.pi / length * product.astype(jnp.float32)
    factor = 1.0 / math.sqrt(length)
    table_real = jnp.cos(angle) * factor
    table_imag = -jnp.sin(angle) * factor
    freq = jnp.where(index < length // 2, index, index - length).astype(jnp.float32)
    theta = -math.pi * chirp_rate / length * (freq[:, None] ** 2 + freq[None, :] ** 2)
    return (table_real, table_imag, jnp.cos(theta), jnp.sin(theta))


def left_product(matrix, field):
    return jnp.einsum(
        "jk,...kl->...jl",
        matrix,
        field,
        preferred_element_type=jnp.float32,
        precision=lax.Precision.HIGHEST,
    )


def right_product(field, matrix):
    return jnp.einsum(
        "...jk,kl->...jl",
        field,
        matrix,
        preferred_element_type=jnp.float32,
        precision=lax.Precision.HIGHEST,
    )


def transform(field, tables, forward):
    table_real = tables[0]
    table_imag = tables[1] if forward else -tables[1]
    real_part = field[..., 0, :, :]
    imag_part = field[..., 1, :, :]
    first_real = left_product(table_real, real_part) - left_product(table_imag, imag_part)
    first_imag = left_product(table_real, imag_part) + left_product(table_imag, real_part)
    out_real = right_product(first_real, table_real) - right_product(first_imag, table_imag)
    out_imag = right_product(first_real, table_imag) + right_product(first_imag, table_real)
    return jnp.stack([out_real, out_imag], axis=-3)


def complex_product(first, second, conjugate):
    first_real = first[..., 0, :, :]
    first_imag = first[..., 1, :, :]
    if conjugate:
        first_imag = -first_imag
    second_real = second[..., 0, :, :]
    second_imag = second[..., 1, :, :]
    return jnp.stack(
        [
            first_real * second_real - first_imag * second_imag,
            first_real * second_imag + first_imag * second_real,
        ],
        axis=-3,
    )


def propagate(field, tables, forward):
    spectrum = transform(field, tables, True)
    sine = tables[3] if forward else -tables[3]
    chirp = jnp.stack([tables[2], sine], axis=0)
    return transform(complex_product(spectrum, chirp, False), tables, False)


def far_field(exit_wave, measured, live, tables):
    spectrum = transform(exit_wave, tables, True)
    power = spectrum[..., 0, :, :] ** 2 + spectrum[..., 1, :, :] ** 2
    keep = live[:, None, None] * (1.0 - measured / jnp.sqrt(power + 1.0))
    residual = spectrum * keep[..., None, :, :]
    return transform(residual, tables, False)


def cut_columns(block, column, width):
    zero = jnp.zeros((), jnp.int32)
    start = (zero,) * (block.ndim - 1) + (column,)
    return lax.dynamic_slice(block, start, block.shape[:-1] + (width,))


def cut_rows(block, row, height):
    zero = jnp.zeros((), jnp.int32)
    start = (zero,) * (block.ndim - 2) + (row, zero)
    return lax.dynamic_slice(block, start, block.shape[:-2] + (height, block.shape[-1]))


def place_columns(block, column, width):
    pad = [(0, 0)] * (block.ndim - 1) + [(width, width - block.shape[-1])]
    return cut_columns(jnp.pad(block, pad), width - column, width)


def pick(stack, index):
    return lax.dynamic_index_in_dim(stack, index, 0, keepdims=False)


def swapped(block, axis):
    return lax.ppermute(block, axis, [(i, i ^ 1) for i in range(lax.axis_size(axis))])


def routed(block, destination):
    tiles = lax.axis_size("scan")
    groups = lax.axis_size("depth")
    route = []
    for t in range(tiles):
        for d in range(groups):
            target = destination(t, d)
            if target is not None:
                route.append((t * groups + d, (target[0] % tiles) * groups + target[1]))
    return lax.ppermute(block, ("scan", "depth"), route)


def body(probe, slices, positions, counts, amplitude):
    patch = probe.shape[-1]
    slots = positions.shape[0]
    layers = slices.shape[0]
    tile_rows = slices.shape[2]
    width = slices.shape[3]
    tables = lax.optimization_barrier(make_tables(patch))
    depth_index = lax.axis_index("depth")
    depth_count = lax.axis_size("depth")
    assert slots == 2 and depth_count % 2 == 0
    pairs = depth_count // 2
    pair = depth_index // 2
    member = depth_index % 2
    span = 2 * layers
    before = shifted(positions, "scan", 1)
    own_rows = slices[:, :, :patch]
    my_row = jnp.where(member == 0, positions[0, 0], positions[1, 0])
    my_column = jnp.where(member == 0, positions[0, 1], positions[1, 1])
    other_column = jnp.where(member == 0, positions[1, 1], positions[0, 1])

    swapped_rows = [swapped(cut_columns(own_rows[layer], other_column, patch), "depth") for layer in range(layers)]
    below = [None] * span
    previous = None
    for source in range(2):
        for layer in range(layers):
            got = []
            for b in range(slots):
                piece = cut_columns(own_rows[layer], before[b, 1], patch)
                if previous is None:
                    probe, piece = lax.optimization_barrier((probe, piece))
                got.append(
                    routed(
                        piece,
                        lambda t, d, b=b, source=source: (t - 1, d - source + b) if d % 2 == source else None,
                    )
                )
            previous = got[0] + got[1]
            below[source * layers + layer] = previous
    path = []
    for j in range(span):
        source = j // layers
        own = cut_columns(own_rows[j % layers], my_column, patch)
        own = jnp.where(member == source, own, swapped_rows[j % layers])
        path.append(cut_rows(jnp.concatenate([own, below[j]], axis=-2), my_row, patch))
    live = (jnp.arange(slots, dtype=jnp.int32) < counts[0]).astype(jnp.float32)
    my_live = jnp.where(member == 0, live[0], live[1])[None]
    my_amplitude = jnp.where(member == 0, amplitude[0], amplitude[1])[None]

    first_psi = propagate(probe[None], tables, True)[0]
    wave_now = None
    saved = []
    for step_number in range(pairs):
        psis = []
        for j in range(span):
            if j == 0 and step_number == 0:
                psi = first_psi
            else:
                psi = propagate(wave_now, tables, True)
            psis.append(psi)
            wave_now = complex_product(psi, path[j], False)
        saved.append(psis)
        if step_number < pairs - 1:
            wave_now = passed_along(wave_now, "depth", 2)
    chi_wave = far_field(wave_now[None], my_amplitude, my_live, tables)[0]

    terms = [None] * pairs
    for step_number in range(pairs - 1, -1, -1):
        found = [None] * span
        for j in range(span - 1, -1, -1):
            found[j] = complex_product(saved[step_number][j], chi_wave, True)
            if j == 0 and step_number == 0:
                continue
            back = complex_product(path[j], chi_wave, True)
            chi_wave = propagate(back, tables, False)
        terms[step_number] = found
        if step_number > 0:
            chi_wave = passed_along(chi_wave, "depth", -2)

    blank = jnp.zeros((2, patch, patch), jnp.float32)
    uppers = [None] * span
    lowers = [[None] * 2 for _ in range(span)]
    swapped_upper = [None] * span
    for j in range(span - 1, -1, -1):
        if pairs == 1:
            mine = terms[0][j]
        else:
            mine = pick(jnp.stack([terms[k][j] for k in range(pairs)], axis=0), pair)
        padded = jnp.concatenate([blank, mine, blank], axis=-2)
        uppers[j] = cut_rows(padded, patch - my_row, patch)
        lower = cut_rows(padded, 2 * patch - my_row, patch)
        owner = j // layers
        for b in range(2):
            lowers[j][b] = routed(
                lower, lambda t, d, b=b, owner=owner: (t + 1, d - b + owner) if d % 2 == b else None
            )
        swapped_upper[j] = routed(
            uppers[j], lambda t, d, owner=owner: (t, d + 2 * owner - 1) if d % 2 == 1 - owner else None
        )
    gradient = []
    for layer in range(layers):
        first, second = layer, layers + layer
        kept = jnp.where(member == 0, uppers[first], uppers[second])
        given = swapped_upper[first] + swapped_upper[second]
        grad = place_columns(kept, my_column, width) + place_columns(given, other_column, width)
        for b in range(2):
            grad = grad + place_columns(lowers[first][b] + lowers[second][b], before[b, 1], width)
        gradient.append(grad)
    return jnp.stack(gradient, axis=0)


def solution(mesh):
    return jax.shard_map(
        body,
        mesh=mesh,
        in_specs=(
            P(),
            P("depth", None, ("groups", "scan"), None),
            P(("groups", "scan"), None),
            P(("groups", "scan")),
            P(("groups", "scan"), None, None),
        ),
        out_specs=P("depth", None, ("groups", "scan"), None),
        check_vma=False,
    )
```

```python
import math

import jax
import jax.numpy as jnp
from jax import lax
from jax.sharding import PartitionSpec as P

chirp_rate = 0.25


def shifted(block, axis, distance):
    devices = range(lax.axis_size(axis))
    route = [((i - distance) % len(devices), i) for i in devices]
    return lax.ppermute(block, axis, route)


def passed_along(block, axis, distance):
    devices = range(lax.axis_size(axis))
    route = [(i - distance, i) for i in devices if i - distance in devices]
    return lax.ppermute(block, axis, route)


def make_tables(length):
    index = jnp.arange(length, dtype=jnp.int32)
    product = index[:, None] * index[None, :] % length
    angle = 2.0 * math.pi / length * product.astype(jnp.float32)
    factor = 1.0 / math.sqrt(length)
    table_real = jnp.cos(angle) * factor
    table_imag = -jnp.sin(angle) * factor
    freq = jnp.where(index < length // 2, index, index - length).astype(jnp.float32)
    theta = -math.pi * chirp_rate / length * (freq[:, None] ** 2 + freq[None, :] ** 2)
    return (table_real, table_imag, jnp.cos(theta), jnp.sin(theta))


def left_product(matrix, field):
    return jnp.einsum(
        "jk,...kl->...jl",
        matrix,
        field,
        preferred_element_type=jnp.float32,
        precision=lax.Precision.HIGHEST,
    )


def right_product(field, matrix):
    return jnp.einsum(
        "...jk,kl->...jl",
        field,
        matrix,
        preferred_element_type=jnp.float32,
        precision=lax.Precision.HIGHEST,
    )


def transform(field, tables, forward):
    table_real = tables[0]
    table_imag = tables[1] if forward else -tables[1]
    real_part = field[..., 0, :, :]
    imag_part = field[..., 1, :, :]
    first_real = left_product(table_real, real_part) - left_product(table_imag, imag_part)
    first_imag = left_product(table_real, imag_part) + left_product(table_imag, real_part)
    out_real = right_product(first_real, table_real) - right_product(first_imag, table_imag)
    out_imag = right_product(first_real, table_imag) + right_product(first_imag, table_real)
    return jnp.stack([out_real, out_imag], axis=-3)


def complex_product(first, second, conjugate):
    first_real = first[..., 0, :, :]
    first_imag = first[..., 1, :, :]
    if conjugate:
        first_imag = -first_imag
    second_real = second[..., 0, :, :]
    second_imag = second[..., 1, :, :]
    return jnp.stack(
        [
            first_real * second_real - first_imag * second_imag,
            first_real * second_imag + first_imag * second_real,
        ],
        axis=-3,
    )


def propagate(field, tables, forward):
    spectrum = transform(field, tables, True)
    sine = tables[3] if forward else -tables[3]
    chirp = jnp.stack([tables[2], sine], axis=0)
    return transform(complex_product(spectrum, chirp, False), tables, False)


def far_field(exit_wave, measured, live, tables):
    spectrum = transform(exit_wave, tables, True)
    power = spectrum[..., 0, :, :] ** 2 + spectrum[..., 1, :, :] ** 2
    keep = live[:, None, None] * (1.0 - measured / jnp.sqrt(power + 1.0))
    residual = spectrum * keep[..., None, :, :]
    return transform(residual, tables, False)


def cut_columns(block, column, width):
    zero = jnp.zeros((), jnp.int32)
    start = (zero,) * (block.ndim - 1) + (column,)
    return lax.dynamic_slice(block, start, block.shape[:-1] + (width,))


def cut_rows(block, row, height):
    zero = jnp.zeros((), jnp.int32)
    start = (zero,) * (block.ndim - 2) + (row, zero)
    return lax.dynamic_slice(block, start, block.shape[:-2] + (height, block.shape[-1]))


def place_columns(block, column, width):
    pad = [(0, 0)] * (block.ndim - 1) + [(width, width - block.shape[-1])]
    return cut_columns(jnp.pad(block, pad), width - column, width)


def pick(stack, index):
    return lax.dynamic_index_in_dim(stack, index, 0, keepdims=False)


def swapped(block, axis):
    return lax.ppermute(block, axis, [(i, i ^ 1) for i in range(lax.axis_size(axis))])


def routed(block, destination):
    tiles = lax.axis_size("scan")
    groups = lax.axis_size("depth")
    route = []
    for t in range(tiles):
        for d in range(groups):
            target = destination(t, d)
            if target is not None:
                route.append((t * groups + d, (target[0] % tiles) * groups + target[1]))
    return lax.ppermute(block, ("scan", "depth"), route)


def body(probe, slices, positions, counts, amplitude):
    patch = probe.shape[-1]
    slots = positions.shape[0]
    layers = slices.shape[0]
    tile_rows = slices.shape[2]
    width = slices.shape[3]
    tables = lax.optimization_barrier(make_tables(patch))
    depth_index = lax.axis_index("depth")
    depth_count = lax.axis_size("depth")
    assert slots == 2 and depth_count % 2 == 0
    pairs = depth_count // 2
    pair = depth_index // 2
    member = depth_index % 2
    span = 2 * layers
    before = shifted(positions, "scan", 1)
    own_rows = slices[:, :, :patch]
    my_row = jnp.where(member == 0, positions[0, 0], positions[1, 0])
    my_column = jnp.where(member == 0, positions[0, 1], positions[1, 1])
    other_column = jnp.where(member == 0, positions[1, 1], positions[0, 1])

    swapped_rows = [swapped(cut_columns(own_rows[layer], other_column, patch), "depth") for layer in range(layers)]
    arrivals = []
    for source in range(2):
        for layer in range(layers):
            got = []
            for b in range(slots):
                piece = cut_columns(own_rows[layer], before[b, 1], patch)
                if not arrivals:
                    probe, piece = lax.optimization_barrier((probe, piece))
                elif len(arrivals) >= 2:
                    piece, arrivals[-2] = lax.optimization_barrier((piece, arrivals[-2]))
                got.append(
                    routed(
                        piece,
                        lambda t, d, b=b, source=source: (t - 1, d - source + b) if d % 2 == source else None,
                    )
                )
            arrivals.append(got[0] + got[1])
    below = arrivals
    path = []
    for j in range(span):
        source = j // layers
        own = cut_columns(own_rows[j % layers], my_column, patch)
        own = jnp.where(member == source, own, swapped_rows[j % layers])
        path.append(cut_rows(jnp.concatenate([own, below[j]], axis=-2), my_row, patch))
    live = (jnp.arange(slots, dtype=jnp.int32) < counts[0]).astype(jnp.float32)
    my_live = jnp.where(member == 0, live[0], live[1])[None]
    my_amplitude = jnp.where(member == 0, amplitude[0], amplitude[1])[None]

    first_psi = propagate(probe[None], tables, True)[0]
    wave_now = None
    saved = []
    for step_number in range(pairs):
        psis = []
        for j in range(span):
            if j == 0 and step_number == 0:
                psi = first_psi
            else:
                psi = propagate(wave_now, tables, True)
            psis.append(psi)
            wave_now = complex_product(psi, path[j], False)
        saved.append(psis)
        if step_number < pairs - 1:
            wave_now = passed_along(wave_now, "depth", 2)
    chi_wave = far_field(wave_now[None], my_amplitude, my_live, tables)[0]

    terms = [None] * pairs
    for step_number in range(pairs - 1, -1, -1):
        found = [None] * span
        for j in range(span - 1, -1, -1):
            found[j] = complex_product(saved[step_number][j], chi_wave, True)
            if j == 0 and step_number == 0:
                continue
            back = complex_product(path[j], chi_wave, True)
            chi_wave = propagate(back, tables, False)
        terms[step_number] = found
        if step_number > 0:
            chi_wave = passed_along(chi_wave, "depth", -2)

    blank = jnp.zeros((2, patch, patch), jnp.float32)
    uppers = [None] * span
    lowers = [[None] * 2 for _ in range(span)]
    swapped_upper = [None] * span
    for j in range(span - 1, -1, -1):
        if pairs == 1:
            mine = terms[0][j]
        else:
            mine = pick(jnp.stack([terms[k][j] for k in range(pairs)], axis=0), pair)
        padded = jnp.concatenate([blank, mine, blank], axis=-2)
        uppers[j] = cut_rows(padded, patch - my_row, patch)
        lower = cut_rows(padded, 2 * patch - my_row, patch)
        owner = j // layers
        for b in range(2):
            lowers[j][b] = routed(
                lower, lambda t, d, b=b, owner=owner: (t + 1, d - b + owner) if d % 2 == b else None
            )
        swapped_upper[j] = routed(
            uppers[j], lambda t, d, owner=owner: (t, d + 2 * owner - 1) if d % 2 == 1 - owner else None
        )
    gradient = []
    for layer in range(layers):
        first, second = layer, layers + layer
        kept = jnp.where(member == 0, uppers[first], uppers[second])
        given = swapped_upper[first] + swapped_upper[second]
        grad = place_columns(kept, my_column, width) + place_columns(given, other_column, width)
        for b in range(2):
            grad = grad + place_columns(lowers[first][b] + lowers[second][b], before[b, 1], width)
        gradient.append(grad)
    return jnp.stack(gradient, axis=0)


def solution(mesh):
    return jax.shard_map(
        body,
        mesh=mesh,
        in_specs=(
            P(),
            P("depth", None, ("groups", "scan"), None),
            P(("groups", "scan"), None),
            P(("groups", "scan")),
            P(("groups", "scan"), None, None),
        ),
        out_specs=P("depth", None, ("groups", "scan"), None),
        check_vma=False,
    )
```

```python
import math

import jax
import jax.numpy as jnp
from jax import lax
from jax.sharding import PartitionSpec as P

chirp_rate = 0.25


def shifted(block, axis, distance):
    devices = range(lax.axis_size(axis))
    route = [((i - distance) % len(devices), i) for i in devices]
    return lax.ppermute(block, axis, route)


def passed_along(block, axis, distance):
    devices = range(lax.axis_size(axis))
    route = [(i - distance, i) for i in devices if i - distance in devices]
    return lax.ppermute(block, axis, route)


def make_tables(length):
    index = jnp.arange(length, dtype=jnp.int32)
    product = index[:, None] * index[None, :] % length
    angle = 2.0 * math.pi / length * product.astype(jnp.float32)
    factor = 1.0 / math.sqrt(length)
    table_real = jnp.cos(angle) * factor
    table_imag = -jnp.sin(angle) * factor
    freq = jnp.where(index < length // 2, index, index - length).astype(jnp.float32)
    theta = -math.pi * chirp_rate / length * (freq[:, None] ** 2 + freq[None, :] ** 2)
    return (table_real, table_imag, jnp.cos(theta), jnp.sin(theta))


def left_product(matrix, field):
    return jnp.einsum(
        "jk,...kl->...jl",
        matrix,
        field,
        preferred_element_type=jnp.float32,
        precision=lax.Precision.HIGHEST,
    )


def right_product(field, matrix):
    return jnp.einsum(
        "...jk,kl->...jl",
        field,
        matrix,
        preferred_element_type=jnp.float32,
        precision=lax.Precision.HIGHEST,
    )


def transform(field, tables, forward):
    table_real = tables[0]
    table_imag = tables[1] if forward else -tables[1]
    real_part = field[..., 0, :, :]
    imag_part = field[..., 1, :, :]
    first_real = left_product(table_real, real_part) - left_product(table_imag, imag_part)
    first_imag = left_product(table_real, imag_part) + left_product(table_imag, real_part)
    out_real = right_product(first_real, table_real) - right_product(first_imag, table_imag)
    out_imag = right_product(first_real, table_imag) + right_product(first_imag, table_real)
    return jnp.stack([out_real, out_imag], axis=-3)


def complex_product(first, second, conjugate):
    first_real = first[..., 0, :, :]
    first_imag = first[..., 1, :, :]
    if conjugate:
        first_imag = -first_imag
    second_real = second[..., 0, :, :]
    second_imag = second[..., 1, :, :]
    return jnp.stack(
        [
            first_real * second_real - first_imag * second_imag,
            first_real * second_imag + first_imag * second_real,
        ],
        axis=-3,
    )


def propagate(field, tables, forward):
    spectrum = transform(field, tables, True)
    sine = tables[3] if forward else -tables[3]
    chirp = jnp.stack([tables[2], sine], axis=0)
    return transform(complex_product(spectrum, chirp, False), tables, False)


def far_field(exit_wave, measured, live, tables):
    spectrum = transform(exit_wave, tables, True)
    power = spectrum[..., 0, :, :] ** 2 + spectrum[..., 1, :, :] ** 2
    keep = live[:, None, None] * (1.0 - measured / jnp.sqrt(power + 1.0))
    residual = spectrum * keep[..., None, :, :]
    return transform(residual, tables, False)


def cut_columns(block, column, width):
    zero = jnp.zeros((), jnp.int32)
    start = (zero,) * (block.ndim - 1) + (column,)
    return lax.dynamic_slice(block, start, block.shape[:-1] + (width,))


def cut_rows(block, row, height):
    zero = jnp.zeros((), jnp.int32)
    start = (zero,) * (block.ndim - 2) + (row, zero)
    return lax.dynamic_slice(block, start, block.shape[:-2] + (height, block.shape[-1]))


def place_columns(block, column, width):
    pad = [(0, 0)] * (block.ndim - 1) + [(width, width - block.shape[-1])]
    return cut_columns(jnp.pad(block, pad), width - column, width)


def pick(stack, index):
    return lax.dynamic_index_in_dim(stack, index, 0, keepdims=False)


def swapped(block, axis):
    return lax.ppermute(block, axis, [(i, i ^ 1) for i in range(lax.axis_size(axis))])


def routed(block, destination):
    tiles = lax.axis_size("scan")
    groups = lax.axis_size("depth")
    route = []
    for t in range(tiles):
        for d in range(groups):
            target = destination(t, d)
            if target is not None:
                route.append((t * groups + d, (target[0] % tiles) * groups + target[1]))
    return lax.ppermute(block, ("scan", "depth"), route)


def body(probe, slices, positions, counts, amplitude):
    patch = probe.shape[-1]
    slots = positions.shape[0]
    layers = slices.shape[0]
    tile_rows = slices.shape[2]
    width = slices.shape[3]
    tables = lax.optimization_barrier(make_tables(patch))
    depth_index = lax.axis_index("depth")
    depth_count = lax.axis_size("depth")
    assert slots == 2 and depth_count % 2 == 0
    pairs = depth_count // 2
    pair = depth_index // 2
    member = depth_index % 2
    span = 2 * layers
    before = shifted(positions, "scan", 1)
    own_rows = slices[:, :, :patch]
    my_row = jnp.where(member == 0, positions[0, 0], positions[1, 0])
    my_column = jnp.where(member == 0, positions[0, 1], positions[1, 1])
    other_column = jnp.where(member == 0, positions[1, 1], positions[0, 1])

    swapped_rows = [swapped(cut_columns(own_rows[layer], other_column, patch), "depth") for layer in range(layers)]
    below = [None] * span
    previous = None
    for source in range(2):
        for layer in range(layers):
            got = []
            for b in range(slots):
                piece = cut_columns(own_rows[layer], before[b, 1], patch)
                if previous is None:
                    probe, piece = lax.optimization_barrier((probe, piece))
                else:
                    piece, previous = lax.optimization_barrier((piece, previous))
                got.append(
                    routed(
                        piece,
                        lambda t, d, b=b, source=source: (t - 1, d - source + b) if d % 2 == source else None,
                    )
                )
            previous = got[0] + got[1]
            below[source * layers + layer] = previous
    path = []
    for j in range(span):
        source = j // layers
        own = cut_columns(own_rows[j % layers], my_column, patch)
        own = jnp.where(member == source, own, swapped_rows[j % layers])
        path.append(cut_rows(jnp.concatenate([own, below[j]], axis=-2), my_row, patch))
    live = (jnp.arange(slots, dtype=jnp.int32) < counts[0]).astype(jnp.float32)
    my_live = jnp.where(member == 0, live[0], live[1])[None]
    my_amplitude = jnp.where(member == 0, amplitude[0], amplitude[1])[None]

    first_psi = propagate(probe[None], tables, True)[0]
    wave_now = None
    saved = []
    for step_number in range(pairs):
        psis = []
        for j in range(span):
            if j == 0 and step_number == 0:
                psi = first_psi
            else:
                psi = propagate(wave_now, tables, True)
            psis.append(psi)
            wave_now = complex_product(psi, path[j], False)
        saved.append(psis)
        if step_number < pairs - 1:
            wave_now = passed_along(wave_now, "depth", 2)
    chi_wave = far_field(wave_now[None], my_amplitude, my_live, tables)[0]

    terms = [None] * pairs
    for step_number in range(pairs - 1, -1, -1):
        found = [None] * span
        for j in range(span - 1, -1, -1):
            found[j] = complex_product(saved[step_number][j], chi_wave, True)
            if j == 0 and step_number == 0:
                continue
            back = complex_product(path[j], chi_wave, True)
            chi_wave = propagate(back, tables, False)
        terms[step_number] = found
        if step_number > 0:
            chi_wave = passed_along(chi_wave, "depth", -2)

    blank = jnp.zeros((2, patch, patch), jnp.float32)
    uppers = [None] * span
    lowers = [[None] * 2 for _ in range(span)]
    swapped_upper = [None] * span
    for j in range(span - 1, -1, -1):
        if pairs == 1:
            mine = terms[0][j]
        else:
            mine = pick(jnp.stack([terms[k][j] for k in range(pairs)], axis=0), pair)
        padded = jnp.concatenate([blank, mine, blank], axis=-2)
        uppers[j] = cut_rows(padded, patch - my_row, patch)
        lower = cut_rows(padded, 2 * patch - my_row, patch)
        owner = j // layers
        for b in range(2):
            lowers[j][b] = routed(
                lower, lambda t, d, b=b, owner=owner: (t + 1, d - b + owner) if d % 2 == b else None
            )
        swapped_upper[j] = routed(
            uppers[j], lambda t, d, owner=owner: (t, d + 2 * owner - 1) if d % 2 == 1 - owner else None
        )
    own = list(range(layers))
    theirs = list(range(layers, span))
    kept = jnp.where(member == 0, jnp.stack([uppers[j] for j in own]), jnp.stack([uppers[j] for j in theirs]))
    given = jnp.stack([swapped_upper[first] + swapped_upper[second] for first, second in zip(own, theirs)])
    gradient = place_columns(kept, my_column, width) + place_columns(given, other_column, width)
    for b in range(2):
        arrived = jnp.stack([lowers[first][b] + lowers[second][b] for first, second in zip(own, theirs)])
        gradient = gradient + place_columns(arrived, before[b, 1], width)
    return gradient


def solution(mesh):
    return jax.shard_map(
        body,
        mesh=mesh,
        in_specs=(
            P(),
            P("depth", None, ("groups", "scan"), None),
            P(("groups", "scan"), None),
            P(("groups", "scan")),
            P(("groups", "scan"), None, None),
        ),
        out_specs=P("depth", None, ("groups", "scan"), None),
        check_vma=False,
    )
```

```python
import math

import jax
import jax.numpy as jnp
from jax import lax
from jax.experimental import pallas as pl
from jax.sharding import PartitionSpec as P

chirp_rate = 0.25


def shifted(block, axis, distance):
    devices = range(lax.axis_size(axis))
    route = [((i - distance) % len(devices), i) for i in devices]
    return lax.ppermute(block, axis, route)


def passed_along(block, axis, distance):
    devices = range(lax.axis_size(axis))
    route = [(i - distance, i) for i in devices if i - distance in devices]
    return lax.ppermute(block, axis, route)


def make_tables(length):
    index = jnp.arange(length, dtype=jnp.int32)
    product = index[:, None] * index[None, :] % length
    angle = 2.0 * math.pi / length * product.astype(jnp.float32)
    factor = 1.0 / math.sqrt(length)
    table_real = jnp.cos(angle) * factor
    table_imag = -jnp.sin(angle) * factor
    freq = jnp.where(index < length // 2, index, index - length).astype(jnp.float32)
    theta = -math.pi * chirp_rate / length * (freq[:, None] ** 2 + freq[None, :] ** 2)
    return (table_real, table_imag, jnp.cos(theta), jnp.sin(theta))


def left_product(matrix, field):
    return jnp.einsum(
        "jk,...kl->...jl",
        matrix,
        field,
        preferred_element_type=jnp.float32,
        precision=lax.Precision.HIGHEST,
    )


def right_product(field, matrix):
    return jnp.einsum(
        "...jk,kl->...jl",
        field,
        matrix,
        preferred_element_type=jnp.float32,
        precision=lax.Precision.HIGHEST,
    )


def transform(field, tables, forward):
    table_real = tables[0]
    table_imag = tables[1] if forward else -tables[1]
    real_part = field[..., 0, :, :]
    imag_part = field[..., 1, :, :]
    first_real = left_product(table_real, real_part) - left_product(table_imag, imag_part)
    first_imag = left_product(table_real, imag_part) + left_product(table_imag, real_part)
    out_real = right_product(first_real, table_real) - right_product(first_imag, table_imag)
    out_imag = right_product(first_real, table_imag) + right_product(first_imag, table_real)
    return jnp.stack([out_real, out_imag], axis=-3)


def complex_product(first, second, conjugate):
    first_real = first[..., 0, :, :]
    first_imag = first[..., 1, :, :]
    if conjugate:
        first_imag = -first_imag
    second_real = second[..., 0, :, :]
    second_imag = second[..., 1, :, :]
    return jnp.stack(
        [
            first_real * second_real - first_imag * second_imag,
            first_real * second_imag + first_imag * second_real,
        ],
        axis=-3,
    )


def propagate_kernel(field_ref, real_ref, imag_ref, cosine_ref, sine_ref, out_ref):
    def dot(a, b):
        return jnp.dot(a, b, precision=lax.Precision.HIGHEST, preferred_element_type=jnp.float32)

    table_real = real_ref[...]
    table_imag = imag_ref[...]
    real_part = field_ref[0]
    imag_part = field_ref[1]
    first_real = dot(table_real, real_part) - dot(table_imag, imag_part)
    first_imag = dot(table_real, imag_part) + dot(table_imag, real_part)
    spectrum_real = dot(first_real, table_real) - dot(first_imag, table_imag)
    spectrum_imag = dot(first_real, table_imag) + dot(first_imag, table_real)
    cosine = cosine_ref[...]
    sine = sine_ref[...]
    chirped_real = spectrum_real * cosine - spectrum_imag * sine
    chirped_imag = spectrum_real * sine + spectrum_imag * cosine
    back_real = dot(table_real, chirped_real) + dot(table_imag, chirped_imag)
    back_imag = dot(table_real, chirped_imag) - dot(table_imag, chirped_real)
    out_ref[0] = dot(back_real, table_real) + dot(back_imag, table_imag)
    out_ref[1] = dot(back_imag, table_real) - dot(back_real, table_imag)


def propagate(field, tables, forward):
    sine = tables[3] if forward else -tables[3]
    if field.ndim == 3:
        return pl.pallas_call(
            propagate_kernel,
            out_shape=jax.ShapeDtypeStruct(field.shape, jnp.float32),
        )(field, tables[0], tables[1], tables[2], sine)
    spectrum = transform(field, tables, True)
    chirp = jnp.stack([tables[2], sine], axis=0)
    return transform(complex_product(spectrum, chirp, False), tables, False)


def far_field(exit_wave, measured, live, tables):
    spectrum = transform(exit_wave, tables, True)
    power = spectrum[..., 0, :, :] ** 2 + spectrum[..., 1, :, :] ** 2
    keep = live[:, None, None] * (1.0 - measured / jnp.sqrt(power + 1.0))
    residual = spectrum * keep[..., None, :, :]
    return transform(residual, tables, False)


def cut_columns(block, column, width):
    zero = jnp.zeros((), jnp.int32)
    start = (zero,) * (block.ndim - 1) + (column,)
    return lax.dynamic_slice(block, start, block.shape[:-1] + (width,))


def cut_rows(block, row, height):
    zero = jnp.zeros((), jnp.int32)
    start = (zero,) * (block.ndim - 2) + (row, zero)
    return lax.dynamic_slice(block, start, block.shape[:-2] + (height, block.shape[-1]))


def place_columns(block, column, width):
    pad = [(0, 0)] * (block.ndim - 1) + [(width, width - block.shape[-1])]
    return cut_columns(jnp.pad(block, pad), width - column, width)


def pick(stack, index):
    return lax.dynamic_index_in_dim(stack, index, 0, keepdims=False)


def swapped(block, axis):
    return lax.ppermute(block, axis, [(i, i ^ 1) for i in range(lax.axis_size(axis))])


def routed(block, destination):
    tiles = lax.axis_size("scan")
    groups = lax.axis_size("depth")
    route = []
    for t in range(tiles):
        for d in range(groups):
            target = destination(t, d)
            if target is not None:
                route.append((t * groups + d, (target[0] % tiles) * groups + target[1]))
    return lax.ppermute(block, ("scan", "depth"), route)


def body(probe, slices, positions, counts, amplitude):
    patch = probe.shape[-1]
    slots = positions.shape[0]
    layers = slices.shape[0]
    tile_rows = slices.shape[2]
    width = slices.shape[3]
    tables = lax.optimization_barrier(make_tables(patch))
    depth_index = lax.axis_index("depth")
    depth_count = lax.axis_size("depth")
    assert slots == 2 and depth_count % 2 == 0
    pairs = depth_count // 2
    pair = depth_index // 2
    member = depth_index % 2
    span = 2 * layers
    before = shifted(positions, "scan", 1)
    own_rows = slices[:, :, :patch]
    my_row = jnp.where(member == 0, positions[0, 0], positions[1, 0])
    my_column = jnp.where(member == 0, positions[0, 1], positions[1, 1])
    other_column = jnp.where(member == 0, positions[1, 1], positions[0, 1])

    swapped_rows = [swapped(cut_columns(own_rows[layer], other_column, patch), "depth") for layer in range(layers)]
    below = [None] * span
    previous = None
    for source in range(2):
        for layer in range(layers):
            got = []
            for b in range(slots):
                piece = cut_columns(own_rows[layer], before[b, 1], patch)
                if previous is None:
                    probe, piece = lax.optimization_barrier((probe, piece))
                else:
                    piece, previous = lax.optimization_barrier((piece, previous))
                got.append(
                    routed(
                        piece,
                        lambda t, d, b=b, source=source: (t - 1, d - source + b) if d % 2 == source else None,
                    )
                )
            previous = got[0] + got[1]
            below[source * layers + layer] = previous
    path = []
    for j in range(span):
        source = j // layers
        own = cut_columns(own_rows[j % layers], my_column, patch)
        own = jnp.where(member == source, own, swapped_rows[j % layers])
        path.append(cut_rows(jnp.concatenate([own, below[j]], axis=-2), my_row, patch))
    live = (jnp.arange(slots, dtype=jnp.int32) < counts[0]).astype(jnp.float32)
    my_live = jnp.where(member == 0, live[0], live[1])[None]
    my_amplitude = jnp.where(member == 0, amplitude[0], amplitude[1])[None]

    first_psi = propagate(probe[None], tables, True)[0]
    wave_now = None
    saved = []
    for step_number in range(pairs):
        psis = []
        for j in range(span):
            if j == 0 and step_number == 0:
                psi = first_psi
            else:
                psi = propagate(wave_now, tables, True)
            psis.append(psi)
            wave_now = complex_product(psi, path[j], False)
        saved.append(psis)
        if step_number < pairs - 1:
            wave_now = passed_along(wave_now, "depth", 2)
    chi_wave = far_field(wave_now[None], my_amplitude, my_live, tables)[0]

    terms = [None] * pairs
    for step_number in range(pairs - 1, -1, -1):
        found = [None] * span
        for j in range(span - 1, -1, -1):
            found[j] = complex_product(saved[step_number][j], chi_wave, True)
            if j == 0 and step_number == 0:
                continue
            back = complex_product(path[j], chi_wave, True)
            chi_wave = propagate(back, tables, False)
        terms[step_number] = found
        if step_number > 0:
            chi_wave = passed_along(chi_wave, "depth", -2)

    blank = jnp.zeros((2, patch, patch), jnp.float32)
    uppers = [None] * span
    lowers = [[None] * 2 for _ in range(span)]
    swapped_upper = [None] * span
    for j in range(span - 1, -1, -1):
        if pairs == 1:
            mine = terms[0][j]
        else:
            mine = pick(jnp.stack([terms[k][j] for k in range(pairs)], axis=0), pair)
        padded = jnp.concatenate([blank, mine, blank], axis=-2)
        uppers[j] = cut_rows(padded, patch - my_row, patch)
        lower = cut_rows(padded, 2 * patch - my_row, patch)
        owner = j // layers
        for b in range(2):
            lowers[j][b] = routed(
                lower, lambda t, d, b=b, owner=owner: (t + 1, d - b + owner) if d % 2 == b else None
            )
        swapped_upper[j] = routed(
            uppers[j], lambda t, d, owner=owner: (t, d + 2 * owner - 1) if d % 2 == 1 - owner else None
        )
    own = list(range(layers))
    theirs = list(range(layers, span))
    kept = jnp.where(member == 0, jnp.stack([uppers[j] for j in own]), jnp.stack([uppers[j] for j in theirs]))
    given = jnp.stack([swapped_upper[first] + swapped_upper[second] for first, second in zip(own, theirs)])
    gradient = place_columns(kept, my_column, width) + place_columns(given, other_column, width)
    for b in range(2):
        arrived = jnp.stack([lowers[first][b] + lowers[second][b] for first, second in zip(own, theirs)])
        gradient = gradient + place_columns(arrived, before[b, 1], width)
    return gradient


def solution(mesh):
    return jax.shard_map(
        body,
        mesh=mesh,
        in_specs=(
            P(),
            P("depth", None, ("groups", "scan"), None),
            P(("groups", "scan"), None),
            P(("groups", "scan")),
            P(("groups", "scan"), None, None),
        ),
        out_specs=P("depth", None, ("groups", "scan"), None),
        check_vma=False,
    )
```

```python
import math

import jax
import jax.numpy as jnp
from jax import lax
from jax.experimental import pallas as pl
from jax.sharding import PartitionSpec as P

chirp_rate = 0.25


def shifted(block, axis, distance):
    devices = range(lax.axis_size(axis))
    route = [((i - distance) % len(devices), i) for i in devices]
    return lax.ppermute(block, axis, route)


def passed_along(block, axis, distance):
    devices = range(lax.axis_size(axis))
    route = [(i - distance, i) for i in devices if i - distance in devices]
    return lax.ppermute(block, axis, route)


def make_tables(length):
    index = jnp.arange(length, dtype=jnp.int32)
    product = index[:, None] * index[None, :] % length
    angle = 2.0 * math.pi / length * product.astype(jnp.float32)
    factor = 1.0 / math.sqrt(length)
    table_real = jnp.cos(angle) * factor
    table_imag = -jnp.sin(angle) * factor
    freq = jnp.where(index < length // 2, index, index - length).astype(jnp.float32)
    theta = -math.pi * chirp_rate / length * (freq[:, None] ** 2 + freq[None, :] ** 2)
    return (table_real, table_imag, jnp.cos(theta), jnp.sin(theta))


def left_product(matrix, field):
    return jnp.einsum(
        "jk,...kl->...jl",
        matrix,
        field,
        preferred_element_type=jnp.float32,
        precision=lax.Precision.HIGHEST,
    )


def right_product(field, matrix):
    return jnp.einsum(
        "...jk,kl->...jl",
        field,
        matrix,
        preferred_element_type=jnp.float32,
        precision=lax.Precision.HIGHEST,
    )


def transform(field, tables, forward):
    table_real = tables[0]
    table_imag = tables[1] if forward else -tables[1]
    real_part = field[..., 0, :, :]
    imag_part = field[..., 1, :, :]
    first_real = left_product(table_real, real_part) - left_product(table_imag, imag_part)
    first_imag = left_product(table_real, imag_part) + left_product(table_imag, real_part)
    out_real = right_product(first_real, table_real) - right_product(first_imag, table_imag)
    out_imag = right_product(first_real, table_imag) + right_product(first_imag, table_real)
    return jnp.stack([out_real, out_imag], axis=-3)


def complex_product(first, second, conjugate):
    first_real = first[..., 0, :, :]
    first_imag = first[..., 1, :, :]
    if conjugate:
        first_imag = -first_imag
    second_real = second[..., 0, :, :]
    second_imag = second[..., 1, :, :]
    return jnp.stack(
        [
            first_real * second_real - first_imag * second_imag,
            first_real * second_imag + first_imag * second_real,
        ],
        axis=-3,
    )


def propagate_kernel(field_ref, real_ref, imag_ref, cosine_ref, sine_ref, out_ref):
    def dot(a, b):
        return jnp.dot(a, b, precision=lax.Precision.HIGHEST, preferred_element_type=jnp.float32)

    table_real = real_ref[...]
    table_imag = imag_ref[...]
    real_part = field_ref[0]
    imag_part = field_ref[1]
    first_real = dot(table_real, real_part) - dot(table_imag, imag_part)
    first_imag = dot(table_real, imag_part) + dot(table_imag, real_part)
    spectrum_real = dot(first_real, table_real) - dot(first_imag, table_imag)
    spectrum_imag = dot(first_real, table_imag) + dot(first_imag, table_real)
    cosine = cosine_ref[...]
    sine = sine_ref[...]
    chirped_real = spectrum_real * cosine - spectrum_imag * sine
    chirped_imag = spectrum_real * sine + spectrum_imag * cosine
    back_real = dot(table_real, chirped_real) + dot(table_imag, chirped_imag)
    back_imag = dot(table_real, chirped_imag) - dot(table_imag, chirped_real)
    out_ref[0] = dot(back_real, table_real) + dot(back_imag, table_imag)
    out_ref[1] = dot(back_imag, table_real) - dot(back_real, table_imag)


def propagate(field, tables, forward):
    sine = tables[3] if forward else -tables[3]
    if field.ndim == 3:
        side = field.shape[-1]
        return pl.pallas_call(
            propagate_kernel,
            out_shape=jax.ShapeDtypeStruct(field.shape, jnp.float32),
            cost_estimate=pl.CostEstimate(
                flops=16 * 2 * 6 * side**3, transcendentals=0, bytes_accessed=4 * 8 * side * side
            ),
        )(field, tables[0], tables[1], tables[2], sine)
    spectrum = transform(field, tables, True)
    chirp = jnp.stack([tables[2], sine], axis=0)
    return transform(complex_product(spectrum, chirp, False), tables, False)


def far_field(exit_wave, measured, live, tables):
    spectrum = transform(exit_wave, tables, True)
    power = spectrum[..., 0, :, :] ** 2 + spectrum[..., 1, :, :] ** 2
    keep = live[:, None, None] * (1.0 - measured / jnp.sqrt(power + 1.0))
    residual = spectrum * keep[..., None, :, :]
    return transform(residual, tables, False)


def cut_columns(block, column, width):
    zero = jnp.zeros((), jnp.int32)
    start = (zero,) * (block.ndim - 1) + (column,)
    return lax.dynamic_slice(block, start, block.shape[:-1] + (width,))


def cut_rows(block, row, height):
    zero = jnp.zeros((), jnp.int32)
    start = (zero,) * (block.ndim - 2) + (row, zero)
    return lax.dynamic_slice(block, start, block.shape[:-2] + (height, block.shape[-1]))


def place_columns(block, column, width):
    pad = [(0, 0)] * (block.ndim - 1) + [(width, width - block.shape[-1])]
    return cut_columns(jnp.pad(block, pad), width - column, width)


def pick(stack, index):
    return lax.dynamic_index_in_dim(stack, index, 0, keepdims=False)


def swapped(block, axis):
    return lax.ppermute(block, axis, [(i, i ^ 1) for i in range(lax.axis_size(axis))])


def routed(block, destination):
    tiles = lax.axis_size("scan")
    groups = lax.axis_size("depth")
    route = []
    for t in range(tiles):
        for d in range(groups):
            target = destination(t, d)
            if target is not None:
                route.append((t * groups + d, (target[0] % tiles) * groups + target[1]))
    return lax.ppermute(block, ("scan", "depth"), route)


def body(probe, slices, positions, counts, amplitude):
    patch = probe.shape[-1]
    slots = positions.shape[0]
    layers = slices.shape[0]
    tile_rows = slices.shape[2]
    width = slices.shape[3]
    tables = lax.optimization_barrier(make_tables(patch))
    depth_index = lax.axis_index("depth")
    depth_count = lax.axis_size("depth")
    assert slots == 2 and depth_count % 2 == 0
    pairs = depth_count // 2
    pair = depth_index // 2
    member = depth_index % 2
    span = 2 * layers
    before = shifted(positions, "scan", 1)
    own_rows = slices[:, :, :patch]
    my_row = jnp.where(member == 0, positions[0, 0], positions[1, 0])
    my_column = jnp.where(member == 0, positions[0, 1], positions[1, 1])
    other_column = jnp.where(member == 0, positions[1, 1], positions[0, 1])

    swapped_rows = [swapped(cut_columns(own_rows[layer], other_column, patch), "depth") for layer in range(layers)]
    below = [None] * span
    previous = None
    for source in range(2):
        for layer in range(layers):
            got = []
            for b in range(slots):
                piece = cut_columns(own_rows[layer], before[b, 1], patch)
                if previous is None:
                    probe, piece = lax.optimization_barrier((probe, piece))
                else:
                    piece, previous = lax.optimization_barrier((piece, previous))
                got.append(
                    routed(
                        piece,
                        lambda t, d, b=b, source=source: (t - 1, d - source + b) if d % 2 == source else None,
                    )
                )
            previous = got[0] + got[1]
            below[source * layers + layer] = previous
    path = []
    for j in range(span):
        source = j // layers
        own = cut_columns(own_rows[j % layers], my_column, patch)
        own = jnp.where(member == source, own, swapped_rows[j % layers])
        path.append(cut_rows(jnp.concatenate([own, below[j]], axis=-2), my_row, patch))
    live = (jnp.arange(slots, dtype=jnp.int32) < counts[0]).astype(jnp.float32)
    my_live = jnp.where(member == 0, live[0], live[1])[None]
    my_amplitude = jnp.where(member == 0, amplitude[0], amplitude[1])[None]

    first_psi = propagate(probe[None], tables, True)[0]
    wave_now = None
    saved = []
    for step_number in range(pairs):
        psis = []
        for j in range(span):
            if j == 0 and step_number == 0:
                psi = first_psi
            else:
                psi = propagate(wave_now, tables, True)
            psis.append(psi)
            wave_now = complex_product(psi, path[j], False)
        saved.append(psis)
        if step_number < pairs - 1:
            wave_now = passed_along(wave_now, "depth", 2)
    chi_wave = far_field(wave_now[None], my_amplitude, my_live, tables)[0]

    terms = [None] * pairs
    for step_number in range(pairs - 1, -1, -1):
        found = [None] * span
        for j in range(span - 1, -1, -1):
            found[j] = complex_product(saved[step_number][j], chi_wave, True)
            if j == 0 and step_number == 0:
                continue
            back = complex_product(path[j], chi_wave, True)
            chi_wave = propagate(back, tables, False)
        terms[step_number] = found
        if step_number > 0:
            chi_wave = passed_along(chi_wave, "depth", -2)

    blank = jnp.zeros((2, patch, patch), jnp.float32)
    uppers = [None] * span
    lowers = [[None] * 2 for _ in range(span)]
    swapped_upper = [None] * span
    for j in range(span - 1, -1, -1):
        if pairs == 1:
            mine = terms[0][j]
        else:
            mine = pick(jnp.stack([terms[k][j] for k in range(pairs)], axis=0), pair)
        padded = jnp.concatenate([blank, mine, blank], axis=-2)
        uppers[j] = cut_rows(padded, patch - my_row, patch)
        lower = cut_rows(padded, 2 * patch - my_row, patch)
        owner = j // layers
        for b in range(2):
            lowers[j][b] = routed(
                lower, lambda t, d, b=b, owner=owner: (t + 1, d - b + owner) if d % 2 == b else None
            )
        swapped_upper[j] = routed(
            uppers[j], lambda t, d, owner=owner: (t, d + 2 * owner - 1) if d % 2 == 1 - owner else None
        )
    own = list(range(layers))
    theirs = list(range(layers, span))
    kept = jnp.where(member == 0, jnp.stack([uppers[j] for j in own]), jnp.stack([uppers[j] for j in theirs]))
    given = jnp.stack([swapped_upper[first] + swapped_upper[second] for first, second in zip(own, theirs)])
    gradient = place_columns(kept, my_column, width) + place_columns(given, other_column, width)
    for b in range(2):
        arrived = jnp.stack([lowers[first][b] + lowers[second][b] for first, second in zip(own, theirs)])
        gradient = gradient + place_columns(arrived, before[b, 1], width)
    return gradient


def solution(mesh):
    return jax.shard_map(
        body,
        mesh=mesh,
        in_specs=(
            P(),
            P("depth", None, ("groups", "scan"), None),
            P(("groups", "scan"), None),
            P(("groups", "scan")),
            P(("groups", "scan"), None, None),
        ),
        out_specs=P("depth", None, ("groups", "scan"), None),
        check_vma=False,
    )
```

```python
import math

import jax
import jax.numpy as jnp
from jax import lax
from jax.experimental import pallas as pl
from jax.sharding import PartitionSpec as P

chirp_rate = 0.25


def shifted(block, axis, distance):
    devices = range(lax.axis_size(axis))
    route = [((i - distance) % len(devices), i) for i in devices]
    return lax.ppermute(block, axis, route)


def passed_along(block, axis, distance):
    devices = range(lax.axis_size(axis))
    route = [(i - distance, i) for i in devices if i - distance in devices]
    return lax.ppermute(block, axis, route)


def make_tables(length):
    index = jnp.arange(length, dtype=jnp.int32)
    product = index[:, None] * index[None, :] % length
    angle = 2.0 * math.pi / length * product.astype(jnp.float32)
    factor = 1.0 / math.sqrt(length)
    table_real = jnp.cos(angle) * factor
    table_imag = -jnp.sin(angle) * factor
    freq = jnp.where(index < length // 2, index, index - length).astype(jnp.float32)
    theta = -math.pi * chirp_rate / length * (freq[:, None] ** 2 + freq[None, :] ** 2)
    return (table_real, table_imag, jnp.cos(theta), jnp.sin(theta))


def left_product(matrix, field):
    return jnp.einsum(
        "jk,...kl->...jl",
        matrix,
        field,
        preferred_element_type=jnp.float32,
        precision=lax.Precision.HIGHEST,
    )


def right_product(field, matrix):
    return jnp.einsum(
        "...jk,kl->...jl",
        field,
        matrix,
        preferred_element_type=jnp.float32,
        precision=lax.Precision.HIGHEST,
    )


def transform(field, tables, forward):
    table_real = tables[0]
    table_imag = tables[1] if forward else -tables[1]
    real_part = field[..., 0, :, :]
    imag_part = field[..., 1, :, :]
    first_real = left_product(table_real, real_part) - left_product(table_imag, imag_part)
    first_imag = left_product(table_real, imag_part) + left_product(table_imag, real_part)
    out_real = right_product(first_real, table_real) - right_product(first_imag, table_imag)
    out_imag = right_product(first_real, table_imag) + right_product(first_imag, table_real)
    return jnp.stack([out_real, out_imag], axis=-3)


def complex_product(first, second, conjugate):
    first_real = first[..., 0, :, :]
    first_imag = first[..., 1, :, :]
    if conjugate:
        first_imag = -first_imag
    second_real = second[..., 0, :, :]
    second_imag = second[..., 1, :, :]
    return jnp.stack(
        [
            first_real * second_real - first_imag * second_imag,
            first_real * second_imag + first_imag * second_real,
        ],
        axis=-3,
    )


def propagate_kernel(field_ref, real_ref, imag_ref, cosine_ref, sine_ref, out_ref):
    def dot(a, b):
        return jnp.dot(a, b, precision=lax.Precision.HIGHEST, preferred_element_type=jnp.float32)

    table_real = real_ref[...]
    table_imag = imag_ref[...]
    real_part = field_ref[0]
    imag_part = field_ref[1]
    first_real = dot(table_real, real_part) - dot(table_imag, imag_part)
    first_imag = dot(table_real, imag_part) + dot(table_imag, real_part)
    spectrum_real = dot(first_real, table_real) - dot(first_imag, table_imag)
    spectrum_imag = dot(first_real, table_imag) + dot(first_imag, table_real)
    cosine = cosine_ref[...]
    sine = sine_ref[...]
    chirped_real = spectrum_real * cosine - spectrum_imag * sine
    chirped_imag = spectrum_real * sine + spectrum_imag * cosine
    back_real = dot(table_real, chirped_real) + dot(table_imag, chirped_imag)
    back_imag = dot(table_real, chirped_imag) - dot(table_imag, chirped_real)
    out_ref[0] = dot(back_real, table_real) + dot(back_imag, table_imag)
    out_ref[1] = dot(back_imag, table_real) - dot(back_real, table_imag)


def propagate(field, tables, forward, fused=True):
    sine = tables[3] if forward else -tables[3]
    if field.ndim == 3 and fused:
        side = field.shape[-1]
        return pl.pallas_call(
            propagate_kernel,
            out_shape=jax.ShapeDtypeStruct(field.shape, jnp.float32),
            cost_estimate=pl.CostEstimate(
                flops=16 * 2 * 6 * side**3, transcendentals=0, bytes_accessed=4 * 8 * side * side
            ),
        )(field, tables[0], tables[1], tables[2], sine)
    spectrum = transform(field, tables, True)
    chirp = jnp.stack([tables[2], sine], axis=0)
    return transform(complex_product(spectrum, chirp, False), tables, False)


def far_field(exit_wave, measured, live, tables):
    spectrum = transform(exit_wave, tables, True)
    power = spectrum[..., 0, :, :] ** 2 + spectrum[..., 1, :, :] ** 2
    keep = live[:, None, None] * (1.0 - measured / jnp.sqrt(power + 1.0))
    residual = spectrum * keep[..., None, :, :]
    return transform(residual, tables, False)


def cut_columns(block, column, width):
    zero = jnp.zeros((), jnp.int32)
    start = (zero,) * (block.ndim - 1) + (column,)
    return lax.dynamic_slice(block, start, block.shape[:-1] + (width,))


def cut_rows(block, row, height):
    zero = jnp.zeros((), jnp.int32)
    start = (zero,) * (block.ndim - 2) + (row, zero)
    return lax.dynamic_slice(block, start, block.shape[:-2] + (height, block.shape[-1]))


def place_columns(block, column, width):
    pad = [(0, 0)] * (block.ndim - 1) + [(width, width - block.shape[-1])]
    return cut_columns(jnp.pad(block, pad), width - column, width)


def pick(stack, index):
    return lax.dynamic_index_in_dim(stack, index, 0, keepdims=False)


def swapped(block, axis):
    return lax.ppermute(block, axis, [(i, i ^ 1) for i in range(lax.axis_size(axis))])


def routed(block, destination):
    tiles = lax.axis_size("scan")
    groups = lax.axis_size("depth")
    route = []
    for t in range(tiles):
        for d in range(groups):
            target = destination(t, d)
            if target is not None:
                route.append((t * groups + d, (target[0] % tiles) * groups + target[1]))
    return lax.ppermute(block, ("scan", "depth"), route)


def body(probe, slices, positions, counts, amplitude):
    patch = probe.shape[-1]
    slots = positions.shape[0]
    layers = slices.shape[0]
    tile_rows = slices.shape[2]
    width = slices.shape[3]
    tables = lax.optimization_barrier(make_tables(patch))
    depth_index = lax.axis_index("depth")
    depth_count = lax.axis_size("depth")
    assert slots == 2 and depth_count % 2 == 0
    pairs = depth_count // 2
    pair = depth_index // 2
    member = depth_index % 2
    span = 2 * layers
    before = shifted(positions, "scan", 1)
    own_rows = slices[:, :, :patch]
    my_row = jnp.where(member == 0, positions[0, 0], positions[1, 0])
    my_column = jnp.where(member == 0, positions[0, 1], positions[1, 1])
    other_column = jnp.where(member == 0, positions[1, 1], positions[0, 1])

    swapped_rows = [swapped(cut_columns(own_rows[layer], other_column, patch), "depth") for layer in range(layers)]
    below = [None] * span
    previous = None
    for source in range(2):
        for layer in range(layers):
            got = []
            for b in range(slots):
                piece = cut_columns(own_rows[layer], before[b, 1], patch)
                if previous is None:
                    probe, piece = lax.optimization_barrier((probe, piece))
                else:
                    piece, previous = lax.optimization_barrier((piece, previous))
                got.append(
                    routed(
                        piece,
                        lambda t, d, b=b, source=source: (t - 1, d - source + b) if d % 2 == source else None,
                    )
                )
            previous = got[0] + got[1]
            below[source * layers + layer] = previous
    path = []
    for j in range(span):
        source = j // layers
        own = cut_columns(own_rows[j % layers], my_column, patch)
        own = jnp.where(member == source, own, swapped_rows[j % layers])
        path.append(cut_rows(jnp.concatenate([own, below[j]], axis=-2), my_row, patch))
    live = (jnp.arange(slots, dtype=jnp.int32) < counts[0]).astype(jnp.float32)
    my_live = jnp.where(member == 0, live[0], live[1])[None]
    my_amplitude = jnp.where(member == 0, amplitude[0], amplitude[1])[None]

    first_psi = propagate(probe[None], tables, True)[0]
    wave_now = None
    saved = []
    for step_number in range(pairs):
        psis = []
        for j in range(span):
            if j == 0 and step_number == 0:
                psi = first_psi
            else:
                psi = propagate(wave_now, tables, True, fused=step_number > 0)
            psis.append(psi)
            wave_now = complex_product(psi, path[j], False)
        saved.append(psis)
        if step_number < pairs - 1:
            wave_now = passed_along(wave_now, "depth", 2)
    chi_wave = far_field(wave_now[None], my_amplitude, my_live, tables)[0]

    terms = [None] * pairs
    for step_number in range(pairs - 1, -1, -1):
        found = [None] * span
        for j in range(span - 1, -1, -1):
            found[j] = complex_product(saved[step_number][j], chi_wave, True)
            if j == 0 and step_number == 0:
                continue
            back = complex_product(path[j], chi_wave, True)
            chi_wave = propagate(back, tables, False)
        terms[step_number] = found
        if step_number > 0:
            chi_wave = passed_along(chi_wave, "depth", -2)

    blank = jnp.zeros((2, patch, patch), jnp.float32)
    uppers = [None] * span
    lowers = [[None] * 2 for _ in range(span)]
    swapped_upper = [None] * span
    for j in range(span - 1, -1, -1):
        if pairs == 1:
            mine = terms[0][j]
        else:
            mine = pick(jnp.stack([terms[k][j] for k in range(pairs)], axis=0), pair)
        padded = jnp.concatenate([blank, mine, blank], axis=-2)
        uppers[j] = cut_rows(padded, patch - my_row, patch)
        lower = cut_rows(padded, 2 * patch - my_row, patch)
        owner = j // layers
        for b in range(2):
            lowers[j][b] = routed(
                lower, lambda t, d, b=b, owner=owner: (t + 1, d - b + owner) if d % 2 == b else None
            )
        swapped_upper[j] = routed(
            uppers[j], lambda t, d, owner=owner: (t, d + 2 * owner - 1) if d % 2 == 1 - owner else None
        )
    own = list(range(layers))
    theirs = list(range(layers, span))
    kept = jnp.where(member == 0, jnp.stack([uppers[j] for j in own]), jnp.stack([uppers[j] for j in theirs]))
    given = jnp.stack([swapped_upper[first] + swapped_upper[second] for first, second in zip(own, theirs)])
    gradient = place_columns(kept, my_column, width) + place_columns(given, other_column, width)
    for b in range(2):
        arrived = jnp.stack([lowers[first][b] + lowers[second][b] for first, second in zip(own, theirs)])
        gradient = gradient + place_columns(arrived, before[b, 1], width)
    return gradient


def solution(mesh):
    return jax.shard_map(
        body,
        mesh=mesh,
        in_specs=(
            P(),
            P("depth", None, ("groups", "scan"), None),
            P(("groups", "scan"), None),
            P(("groups", "scan")),
            P(("groups", "scan"), None, None),
        ),
        out_specs=P("depth", None, ("groups", "scan"), None),
        check_vma=False,
    )
```

```python
import math

import jax
import jax.numpy as jnp
from jax import lax
from jax.sharding import PartitionSpec as P

chirp_rate = 0.25


def shifted(block, axis, distance):
    devices = range(lax.axis_size(axis))
    route = [((i - distance) % len(devices), i) for i in devices]
    return lax.ppermute(block, axis, route)


def passed_along(block, axis, distance):
    devices = range(lax.axis_size(axis))
    route = [(i - distance, i) for i in devices if i - distance in devices]
    return lax.ppermute(block, axis, route)


def make_tables(length):
    index = jnp.arange(length, dtype=jnp.int32)
    product = index[:, None] * index[None, :] % length
    angle = 2.0 * math.pi / length * product.astype(jnp.float32)
    factor = 1.0 / math.sqrt(length)
    table_real = jnp.cos(angle) * factor
    table_imag = -jnp.sin(angle) * factor
    freq = jnp.where(index < length // 2, index, index - length).astype(jnp.float32)
    theta = -math.pi * chirp_rate / length * (freq[:, None] ** 2 + freq[None, :] ** 2)
    return (table_real, table_imag, jnp.cos(theta), jnp.sin(theta))


def left_product(matrix, field):
    return jnp.einsum(
        "jk,...kl->...jl",
        matrix,
        field,
        preferred_element_type=jnp.float32,
        precision=lax.Precision.HIGHEST,
    )


def right_product(field, matrix):
    return jnp.einsum(
        "...jk,kl->...jl",
        field,
        matrix,
        preferred_element_type=jnp.float32,
        precision=lax.Precision.HIGHEST,
    )


def transform(field, tables, forward):
    table_real = tables[0]
    table_imag = tables[1] if forward else -tables[1]
    real_part = field[..., 0, :, :]
    imag_part = field[..., 1, :, :]
    first_real = left_product(table_real, real_part) - left_product(table_imag, imag_part)
    first_imag = left_product(table_real, imag_part) + left_product(table_imag, real_part)
    out_real = right_product(first_real, table_real) - right_product(first_imag, table_imag)
    out_imag = right_product(first_real, table_imag) + right_product(first_imag, table_real)
    return jnp.stack([out_real, out_imag], axis=-3)


def complex_product(first, second, conjugate):
    first_real = first[..., 0, :, :]
    first_imag = first[..., 1, :, :]
    if conjugate:
        first_imag = -first_imag
    second_real = second[..., 0, :, :]
    second_imag = second[..., 1, :, :]
    return jnp.stack(
        [
            first_real * second_real - first_imag * second_imag,
            first_real * second_imag + first_imag * second_real,
        ],
        axis=-3,
    )


def propagate(field, tables, forward):
    spectrum = transform(field, tables, True)
    sine = tables[3] if forward else -tables[3]
    chirp = jnp.stack([tables[2], sine], axis=0)
    return transform(complex_product(spectrum, chirp, False), tables, False)


def far_field(exit_wave, measured, live, tables):
    spectrum = transform(exit_wave, tables, True)
    power = spectrum[..., 0, :, :] ** 2 + spectrum[..., 1, :, :] ** 2
    keep = live[:, None, None] * (1.0 - measured / jnp.sqrt(power + 1.0))
    residual = spectrum * keep[..., None, :, :]
    return transform(residual, tables, False)


def cut_columns(block, column, width):
    zero = jnp.zeros((), jnp.int32)
    start = (zero,) * (block.ndim - 1) + (column,)
    return lax.dynamic_slice(block, start, block.shape[:-1] + (width,))


def cut_rows(block, row, height):
    zero = jnp.zeros((), jnp.int32)
    start = (zero,) * (block.ndim - 2) + (row, zero)
    return lax.dynamic_slice(block, start, block.shape[:-2] + (height, block.shape[-1]))


def place_columns(block, column, width):
    pad = [(0, 0)] * (block.ndim - 1) + [(width, width - block.shape[-1])]
    return cut_columns(jnp.pad(block, pad), width - column, width)


def pick(stack, index):
    return lax.dynamic_index_in_dim(stack, index, 0, keepdims=False)


def swapped(block, axis):
    return lax.ppermute(block, axis, [(i, i ^ 1) for i in range(lax.axis_size(axis))])


def routed(block, destination):
    tiles = lax.axis_size("scan")
    groups = lax.axis_size("depth")
    route = []
    for t in range(tiles):
        for d in range(groups):
            target = destination(t, d)
            if target is not None:
                route.append((t * groups + d, (target[0] % tiles) * groups + target[1]))
    return lax.ppermute(block, ("scan", "depth"), route)


def body(probe, slices, positions, counts, amplitude):
    patch = probe.shape[-1]
    slots = positions.shape[0]
    layers = slices.shape[0]
    tile_rows = slices.shape[2]
    width = slices.shape[3]
    tables = lax.optimization_barrier(make_tables(patch))
    depth_index = lax.axis_index("depth")
    depth_count = lax.axis_size("depth")
    assert slots == 2 and depth_count % 2 == 0
    pairs = depth_count // 2
    pair = depth_index // 2
    member = depth_index % 2
    span = 2 * layers
    before = shifted(positions, "scan", 1)
    own_rows = slices[:, :, :patch]
    my_row = jnp.where(member == 0, positions[0, 0], positions[1, 0])
    my_column = jnp.where(member == 0, positions[0, 1], positions[1, 1])
    other_column = jnp.where(member == 0, positions[1, 1], positions[0, 1])

    swapped_rows = [swapped(cut_columns(own_rows[layer], other_column, patch), "depth") for layer in range(layers)]
    below = [None] * span
    previous = None
    for source in range(2):
        for layer in range(layers):
            got = []
            for b in range(slots):
                piece = cut_columns(own_rows[layer], before[b, 1], patch)
                if previous is None:
                    probe, piece = lax.optimization_barrier((probe, piece))
                else:
                    piece, previous = lax.optimization_barrier((piece, previous))
                got.append(
                    routed(
                        piece,
                        lambda t, d, b=b, source=source: (t - 1, d - source + b) if d % 2 == source else None,
                    )
                )
            previous = got[0] + got[1]
            below[source * layers + layer] = previous
    path = []
    for j in range(span):
        source = j // layers
        own = cut_columns(own_rows[j % layers], my_column, patch)
        own = jnp.where(member == source, own, swapped_rows[j % layers])
        path.append(cut_rows(jnp.concatenate([own, below[j]], axis=-2), my_row, patch))
    live = (jnp.arange(slots, dtype=jnp.int32) < counts[0]).astype(jnp.float32)
    my_live = jnp.where(member == 0, live[0], live[1])[None]
    my_amplitude = jnp.where(member == 0, amplitude[0], amplitude[1])[None]

    first_psi = propagate(probe[None], tables, True)[0]
    wave_now = None
    saved = []
    for step_number in range(pairs):
        psis = []
        for j in range(span):
            if j == 0 and step_number == 0:
                psi = first_psi
            else:
                psi = propagate(wave_now, tables, True)
            psis.append(psi)
            wave_now = complex_product(psi, path[j], False)
        saved.append(psis)
        if step_number < pairs - 1:
            wave_now = passed_along(wave_now, "depth", 2)
    chi_wave = far_field(wave_now[None], my_amplitude, my_live, tables)[0]

    blank = jnp.zeros((2, patch, patch), jnp.float32)
    uppers = [None] * span
    lowers = [[None] * 2 for _ in range(span)]
    swapped_upper = [None] * span
    terms = [[None] * span for _ in range(pairs)]

    def send_terms(j):
        if pairs == 1:
            mine = terms[0][j]
        else:
            mine = pick(jnp.stack([terms[k][j] for k in range(pairs)], axis=0), pair)
        padded = jnp.concatenate([blank, mine, blank], axis=-2)
        uppers[j] = cut_rows(padded, patch - my_row, patch)
        lower = cut_rows(padded, 2 * patch - my_row, patch)
        owner = j // layers
        for b in range(2):
            lowers[j][b] = routed(
                lower, lambda t, d, b=b, owner=owner: (t + 1, d - b + owner) if d % 2 == b else None
            )
        swapped_upper[j] = routed(
            uppers[j], lambda t, d, owner=owner: (t, d + 2 * owner - 1) if d % 2 == 1 - owner else None
        )

    for step_number in range(pairs - 1, -1, -1):
        for j in range(span - 1, -1, -1):
            terms[step_number][j] = complex_product(saved[step_number][j], chi_wave, True)
            if step_number == 0:
                send_terms(j)
            if j == 0 and step_number == 0:
                continue
            back = complex_product(path[j], chi_wave, True)
            if step_number == 0 and j + 2 < span:
                done = (lowers[j + 2][0], lowers[j + 2][1], swapped_upper[j + 2])
                back, done = lax.optimization_barrier((back, done))
                lowers[j + 2][0], lowers[j + 2][1], swapped_upper[j + 2] = done
            chi_wave = propagate(back, tables, False)
        if step_number > 0:
            chi_wave = passed_along(chi_wave, "depth", -2)

    own = list(range(layers))
    theirs = list(range(layers, span))
    kept = jnp.where(member == 0, jnp.stack([uppers[j] for j in own]), jnp.stack([uppers[j] for j in theirs]))
    given = jnp.stack([swapped_upper[first] + swapped_upper[second] for first, second in zip(own, theirs)])
    gradient = place_columns(kept, my_column, width) + place_columns(given, other_column, width)
    for b in range(2):
        arrived = jnp.stack([lowers[first][b] + lowers[second][b] for first, second in zip(own, theirs)])
        gradient = gradient + place_columns(arrived, before[b, 1], width)
    return gradient


def solution(mesh):
    return jax.shard_map(
        body,
        mesh=mesh,
        in_specs=(
            P(),
            P("depth", None, ("groups", "scan"), None),
            P(("groups", "scan"), None),
            P(("groups", "scan")),
            P(("groups", "scan"), None, None),
        ),
        out_specs=P("depth", None, ("groups", "scan"), None),
        check_vma=False,
    )
```

```python
import math

import jax
import jax.numpy as jnp
from jax import lax
from jax.sharding import PartitionSpec as P

chirp_rate = 0.25


def shifted(block, axis, distance):
    devices = range(lax.axis_size(axis))
    route = [((i - distance) % len(devices), i) for i in devices]
    return lax.ppermute(block, axis, route)


def passed_along(block, axis, distance):
    devices = range(lax.axis_size(axis))
    route = [(i - distance, i) for i in devices if i - distance in devices]
    return lax.ppermute(block, axis, route)


def make_tables(length):
    index = jnp.arange(length, dtype=jnp.int32)
    product = index[:, None] * index[None, :] % length
    angle = 2.0 * math.pi / length * product.astype(jnp.float32)
    factor = 1.0 / math.sqrt(length)
    table_real = jnp.cos(angle) * factor
    table_imag = -jnp.sin(angle) * factor
    freq = jnp.where(index < length // 2, index, index - length).astype(jnp.float32)
    theta = -math.pi * chirp_rate / length * (freq[:, None] ** 2 + freq[None, :] ** 2)
    return (table_real, table_imag, jnp.cos(theta), jnp.sin(theta))


def left_product(matrix, field):
    return jnp.einsum(
        "jk,...kl->...jl",
        matrix,
        field,
        preferred_element_type=jnp.float32,
        precision=lax.Precision.HIGHEST,
    )


def right_product(field, matrix):
    return jnp.einsum(
        "...jk,kl->...jl",
        field,
        matrix,
        preferred_element_type=jnp.float32,
        precision=lax.Precision.HIGHEST,
    )


def transform(field, tables, forward):
    table_real = tables[0]
    table_imag = tables[1] if forward else -tables[1]
    real_part = field[..., 0, :, :]
    imag_part = field[..., 1, :, :]
    first_real = left_product(table_real, real_part) - left_product(table_imag, imag_part)
    first_imag = left_product(table_real, imag_part) + left_product(table_imag, real_part)
    out_real = right_product(first_real, table_real) - right_product(first_imag, table_imag)
    out_imag = right_product(first_real, table_imag) + right_product(first_imag, table_real)
    return jnp.stack([out_real, out_imag], axis=-3)


def complex_product(first, second, conjugate):
    first_real = first[..., 0, :, :]
    first_imag = first[..., 1, :, :]
    if conjugate:
        first_imag = -first_imag
    second_real = second[..., 0, :, :]
    second_imag = second[..., 1, :, :]
    return jnp.stack(
        [
            first_real * second_real - first_imag * second_imag,
            first_real * second_imag + first_imag * second_real,
        ],
        axis=-3,
    )


def propagate(field, tables, forward):
    spectrum = transform(field, tables, True)
    sine = tables[3] if forward else -tables[3]
    chirp = jnp.stack([tables[2], sine], axis=0)
    return transform(complex_product(spectrum, chirp, False), tables, False)


def far_field(exit_wave, measured, live, tables):
    spectrum = transform(exit_wave, tables, True)
    power = spectrum[..., 0, :, :] ** 2 + spectrum[..., 1, :, :] ** 2
    keep = live[:, None, None] * (1.0 - measured / jnp.sqrt(power + 1.0))
    residual = spectrum * keep[..., None, :, :]
    return transform(residual, tables, False)


def cut_columns(block, column, width):
    zero = jnp.zeros((), jnp.int32)
    start = (zero,) * (block.ndim - 1) + (column,)
    return lax.dynamic_slice(block, start, block.shape[:-1] + (width,))


def cut_rows(block, row, height):
    zero = jnp.zeros((), jnp.int32)
    start = (zero,) * (block.ndim - 2) + (row, zero)
    return lax.dynamic_slice(block, start, block.shape[:-2] + (height, block.shape[-1]))


def place_columns(block, column, width):
    pad = [(0, 0)] * (block.ndim - 1) + [(width, width - block.shape[-1])]
    return cut_columns(jnp.pad(block, pad), width - column, width)


def pick(stack, index):
    return lax.dynamic_index_in_dim(stack, index, 0, keepdims=False)


def swapped(block, axis):
    return lax.ppermute(block, axis, [(i, i ^ 1) for i in range(lax.axis_size(axis))])


def routed(block, destination):
    tiles = lax.axis_size("scan")
    groups = lax.axis_size("depth")
    route = []
    for t in range(tiles):
        for d in range(groups):
            target = destination(t, d)
            if target is not None:
                route.append((t * groups + d, (target[0] % tiles) * groups + target[1]))
    return lax.ppermute(block, ("scan", "depth"), route)


def body(probe, slices, positions, counts, amplitude):
    patch = probe.shape[-1]
    slots = positions.shape[0]
    layers = slices.shape[0]
    tile_rows = slices.shape[2]
    width = slices.shape[3]
    tables = lax.optimization_barrier(make_tables(patch))
    depth_index = lax.axis_index("depth")
    depth_count = lax.axis_size("depth")
    assert slots == 2 and depth_count % 2 == 0
    pairs = depth_count // 2
    pair = depth_index // 2
    member = depth_index % 2
    span = 2 * layers
    before = shifted(positions, "scan", 1)
    own_rows = slices[:, :, :patch]
    my_row = jnp.where(member == 0, positions[0, 0], positions[1, 0])
    my_column = jnp.where(member == 0, positions[0, 1], positions[1, 1])
    other_column = jnp.where(member == 0, positions[1, 1], positions[0, 1])

    swapped_rows = [swapped(cut_columns(own_rows[layer], other_column, patch), "depth") for layer in range(layers)]
    below = [None] * span
    previous = None
    for source in range(2):
        for layer in range(layers):
            got = []
            for b in range(slots):
                piece = cut_columns(own_rows[layer], before[b, 1], patch)
                if previous is None:
                    probe, piece = lax.optimization_barrier((probe, piece))
                else:
                    piece, previous = lax.optimization_barrier((piece, previous))
                got.append(
                    routed(
                        piece,
                        lambda t, d, b=b, source=source: (t - 1, d - source + b) if d % 2 == source else None,
                    )
                )
            previous = got[0] + got[1]
            below[source * layers + layer] = previous
    path = []
    for j in range(span):
        source = j // layers
        own = cut_columns(own_rows[j % layers], my_column, patch)
        own = jnp.where(member == source, own, swapped_rows[j % layers])
        path.append(cut_rows(jnp.concatenate([own, below[j]], axis=-2), my_row, patch))
    live = (jnp.arange(slots, dtype=jnp.int32) < counts[0]).astype(jnp.float32)
    my_live = jnp.where(member == 0, live[0], live[1])[None]
    my_amplitude = jnp.where(member == 0, amplitude[0], amplitude[1])[None]

    first_psi = propagate(probe[None], tables, True)[0]
    wave_now = None
    saved = []
    for step_number in range(pairs):
        psis = []
        for j in range(span):
            if j == 0 and step_number == 0:
                psi = first_psi
            else:
                psi = propagate(wave_now, tables, True)
            psis.append(psi)
            wave_now = complex_product(psi, path[j], False)
        saved.append(psis)
        if step_number < pairs - 1:
            wave_now = passed_along(wave_now, "depth", 2)
    chi_wave = far_field(wave_now[None], my_amplitude, my_live, tables)[0]

    blank = jnp.zeros((2, patch, patch), jnp.float32)
    uppers = [None] * span
    lowers = [[None] * 2 for _ in range(span)]
    swapped_upper = [None] * span
    terms = [[None] * span for _ in range(pairs)]

    def send_terms(j):
        if pairs == 1:
            mine = terms[0][j]
        else:
            mine = pick(jnp.stack([terms[k][j] for k in range(pairs)], axis=0), pair)
        padded = jnp.concatenate([blank, mine, blank], axis=-2)
        uppers[j] = cut_rows(padded, patch - my_row, patch)
        lower = cut_rows(padded, 2 * patch - my_row, patch)
        owner = j // layers
        for b in range(2):
            lowers[j][b] = routed(
                lower, lambda t, d, b=b, owner=owner: (t + 1, d - b + owner) if d % 2 == b else None
            )
        swapped_upper[j] = routed(
            uppers[j], lambda t, d, owner=owner: (t, d + 2 * owner - 1) if d % 2 == 1 - owner else None
        )

    for step_number in range(pairs - 1, -1, -1):
        for j in range(span - 1, -1, -1):
            if step_number == 0 and j == 0 and span > 2:
                done = (lowers[2][0], lowers[2][1], swapped_upper[2])
                chi_wave, done = lax.optimization_barrier((chi_wave, done))
                lowers[2][0], lowers[2][1], swapped_upper[2] = done
            terms[step_number][j] = complex_product(saved[step_number][j], chi_wave, True)
            if step_number == 0:
                send_terms(j)
            if j == 0 and step_number == 0:
                continue
            back = complex_product(path[j], chi_wave, True)
            if step_number == 0 and j + 2 < span:
                done = (lowers[j + 2][0], lowers[j + 2][1], swapped_upper[j + 2])
                back, done = lax.optimization_barrier((back, done))
                lowers[j + 2][0], lowers[j + 2][1], swapped_upper[j + 2] = done
            chi_wave = propagate(back, tables, False)
        if step_number > 0:
            chi_wave = passed_along(chi_wave, "depth", -2)

    own = list(range(layers))
    theirs = list(range(layers, span))
    kept = jnp.where(member == 0, jnp.stack([uppers[j] for j in own]), jnp.stack([uppers[j] for j in theirs]))
    given = jnp.stack([swapped_upper[first] + swapped_upper[second] for first, second in zip(own, theirs)])
    gradient = place_columns(kept, my_column, width) + place_columns(given, other_column, width)
    for b in range(2):
        arrived = jnp.stack([lowers[first][b] + lowers[second][b] for first, second in zip(own, theirs)])
        gradient = gradient + place_columns(arrived, before[b, 1], width)
    return gradient


def solution(mesh):
    return jax.shard_map(
        body,
        mesh=mesh,
        in_specs=(
            P(),
            P("depth", None, ("groups", "scan"), None),
            P(("groups", "scan"), None),
            P(("groups", "scan")),
            P(("groups", "scan"), None, None),
        ),
        out_specs=P("depth", None, ("groups", "scan"), None),
        check_vma=False,
    )
```

```python
import math

import jax
import jax.numpy as jnp
from jax import lax
from jax.sharding import PartitionSpec as P

chirp_rate = 0.25


def shifted(block, axis, distance):
    devices = range(lax.axis_size(axis))
    route = [((i - distance) % len(devices), i) for i in devices]
    return lax.ppermute(block, axis, route)


def passed_along(block, axis, distance):
    devices = range(lax.axis_size(axis))
    route = [(i - distance, i) for i in devices if i - distance in devices]
    return lax.ppermute(block, axis, route)


def make_tables(length):
    index = jnp.arange(length, dtype=jnp.int32)
    product = index[:, None] * index[None, :] % length
    angle = 2.0 * math.pi / length * product.astype(jnp.float32)
    factor = 1.0 / math.sqrt(length)
    table_real = jnp.cos(angle) * factor
    table_imag = -jnp.sin(angle) * factor
    freq = jnp.where(index < length // 2, index, index - length).astype(jnp.float32)
    theta = -math.pi * chirp_rate / length * (freq[:, None] ** 2 + freq[None, :] ** 2)
    return (table_real, table_imag, jnp.cos(theta), jnp.sin(theta))


def left_product(matrix, field):
    return jnp.einsum(
        "jk,...kl->...jl",
        matrix,
        field,
        preferred_element_type=jnp.float32,
        precision=lax.Precision.HIGHEST,
    )


def right_product(field, matrix):
    return jnp.einsum(
        "...jk,kl->...jl",
        field,
        matrix,
        preferred_element_type=jnp.float32,
        precision=lax.Precision.HIGHEST,
    )


def transform(field, tables, forward):
    table_real = tables[0]
    table_imag = tables[1] if forward else -tables[1]
    real_part = field[..., 0, :, :]
    imag_part = field[..., 1, :, :]
    first_real = left_product(table_real, real_part) - left_product(table_imag, imag_part)
    first_imag = left_product(table_real, imag_part) + left_product(table_imag, real_part)
    out_real = right_product(first_real, table_real) - right_product(first_imag, table_imag)
    out_imag = right_product(first_real, table_imag) + right_product(first_imag, table_real)
    return jnp.stack([out_real, out_imag], axis=-3)


def complex_product(first, second, conjugate):
    first_real = first[..., 0, :, :]
    first_imag = first[..., 1, :, :]
    if conjugate:
        first_imag = -first_imag
    second_real = second[..., 0, :, :]
    second_imag = second[..., 1, :, :]
    return jnp.stack(
        [
            first_real * second_real - first_imag * second_imag,
            first_real * second_imag + first_imag * second_real,
        ],
        axis=-3,
    )


def propagate(field, tables, forward):
    spectrum = transform(field, tables, True)
    sine = tables[3] if forward else -tables[3]
    chirp = jnp.stack([tables[2], sine], axis=0)
    return transform(complex_product(spectrum, chirp, False), tables, False)


def far_field(exit_wave, measured, live, tables):
    spectrum = transform(exit_wave, tables, True)
    power = spectrum[..., 0, :, :] ** 2 + spectrum[..., 1, :, :] ** 2
    keep = live[:, None, None] * (1.0 - measured / jnp.sqrt(power + 1.0))
    residual = spectrum * keep[..., None, :, :]
    return transform(residual, tables, False)


def cut_columns(block, column, width):
    zero = jnp.zeros((), jnp.int32)
    start = (zero,) * (block.ndim - 1) + (column,)
    return lax.dynamic_slice(block, start, block.shape[:-1] + (width,))


def cut_rows(block, row, height):
    zero = jnp.zeros((), jnp.int32)
    start = (zero,) * (block.ndim - 2) + (row, zero)
    return lax.dynamic_slice(block, start, block.shape[:-2] + (height, block.shape[-1]))


def place_columns(block, column, width):
    pad = [(0, 0)] * (block.ndim - 1) + [(width, width - block.shape[-1])]
    return cut_columns(jnp.pad(block, pad), width - column, width)


def pick(stack, index):
    return lax.dynamic_index_in_dim(stack, index, 0, keepdims=False)


def swapped(block, axis):
    return lax.ppermute(block, axis, [(i, i ^ 1) for i in range(lax.axis_size(axis))])


def routed(block, destination):
    tiles = lax.axis_size("scan")
    groups = lax.axis_size("depth")
    route = []
    for t in range(tiles):
        for d in range(groups):
            target = destination(t, d)
            if target is not None:
                route.append((t * groups + d, (target[0] % tiles) * groups + target[1]))
    return lax.ppermute(block, ("scan", "depth"), route)


def body(probe, slices, positions, counts, amplitude):
    patch = probe.shape[-1]
    slots = positions.shape[0]
    layers = slices.shape[0]
    tile_rows = slices.shape[2]
    width = slices.shape[3]
    tables = lax.optimization_barrier(make_tables(patch))
    depth_index = lax.axis_index("depth")
    depth_count = lax.axis_size("depth")
    assert slots == 2 and depth_count % 2 == 0
    pairs = depth_count // 2
    pair = depth_index // 2
    member = depth_index % 2
    span = 2 * layers
    before = shifted(positions, "scan", 1)
    own_rows = slices[:, :, :patch]
    my_row = jnp.where(member == 0, positions[0, 0], positions[1, 0])
    my_column = jnp.where(member == 0, positions[0, 1], positions[1, 1])
    other_column = jnp.where(member == 0, positions[1, 1], positions[0, 1])

    swapped_rows = [swapped(cut_columns(own_rows[layer], other_column, patch), "depth") for layer in range(layers)]
    below = [None] * span
    previous = None
    for source in range(2):
        for layer in range(layers):
            got = []
            for b in range(slots):
                piece = cut_columns(own_rows[layer], before[b, 1], patch)
                if previous is None:
                    probe, piece = lax.optimization_barrier((probe, piece))
                else:
                    piece, previous = lax.optimization_barrier((piece, previous))
                got.append(
                    routed(
                        piece,
                        lambda t, d, b=b, source=source: (t - 1, d - source + b) if d % 2 == source else None,
                    )
                )
            previous = got[0] + got[1]
            below[source * layers + layer] = previous
    path = []
    for j in range(span):
        source = j // layers
        own = cut_columns(own_rows[j % layers], my_column, patch)
        own = jnp.where(member == source, own, swapped_rows[j % layers])
        path.append(cut_rows(jnp.concatenate([own, below[j]], axis=-2), my_row, patch))
    live = (jnp.arange(slots, dtype=jnp.int32) < counts[0]).astype(jnp.float32)
    my_live = jnp.where(member == 0, live[0], live[1])[None]
    my_amplitude = jnp.where(member == 0, amplitude[0], amplitude[1])[None]

    first_psi = propagate(probe[None], tables, True)[0]
    wave_now = None
    saved = []
    for step_number in range(pairs):
        psis = []
        for j in range(span):
            if j == 0 and step_number == 0:
                psi = first_psi
            else:
                psi = propagate(wave_now, tables, True)
            psis.append(psi)
            wave_now = complex_product(psi, path[j], False)
        saved.append(psis)
        if step_number < pairs - 1:
            wave_now = passed_along(wave_now, "depth", 2)
    chi_wave = far_field(wave_now[None], my_amplitude, my_live, tables)[0]

    blank = jnp.zeros((2, patch, patch), jnp.float32)
    uppers = [None] * span
    lowers = [[None] * 2 for _ in range(span)]
    swapped_upper = [None] * span
    terms = [[None] * span for _ in range(pairs)]

    def send_terms(j):
        if pairs == 1:
            mine = terms[0][j]
        else:
            mine = pick(jnp.stack([terms[k][j] for k in range(pairs)], axis=0), pair)
        padded = jnp.concatenate([blank, mine, blank], axis=-2)
        uppers[j] = cut_rows(padded, patch - my_row, patch)
        lower = cut_rows(padded, 2 * patch - my_row, patch)
        owner = j // layers
        for b in range(2):
            lowers[j][b] = routed(
                lower, lambda t, d, b=b, owner=owner: (t + 1, d - b + owner) if d % 2 == b else None
            )
        swapped_upper[j] = routed(
            uppers[j], lambda t, d, owner=owner: (t, d + 2 * owner - 1) if d % 2 == 1 - owner else None
        )

    for step_number in range(pairs - 1, -1, -1):
        for j in range(span - 1, -1, -1):
            if step_number == 0 and j == 0 and span > 2:
                done = tuple((lowers[k][0], lowers[k][1], swapped_upper[k]) for k in (1, 2))
                chi_wave, done = lax.optimization_barrier((chi_wave, done))
                for k, sent in zip((1, 2), done):
                    lowers[k][0], lowers[k][1], swapped_upper[k] = sent
            terms[step_number][j] = complex_product(saved[step_number][j], chi_wave, True)
            if step_number == 0:
                send_terms(j)
            if j == 0 and step_number == 0:
                continue
            back = complex_product(path[j], chi_wave, True)
            if step_number == 0 and j + 2 < span:
                done = (lowers[j + 2][0], lowers[j + 2][1], swapped_upper[j + 2])
                back, done = lax.optimization_barrier((back, done))
                lowers[j + 2][0], lowers[j + 2][1], swapped_upper[j + 2] = done
            chi_wave = propagate(back, tables, False)
        if step_number > 0:
            chi_wave = passed_along(chi_wave, "depth", -2)

    own = list(range(layers))
    theirs = list(range(layers, span))
    kept = jnp.where(member == 0, jnp.stack([uppers[j] for j in own]), jnp.stack([uppers[j] for j in theirs]))
    given = jnp.stack([swapped_upper[first] + swapped_upper[second] for first, second in zip(own, theirs)])
    gradient = place_columns(kept, my_column, width) + place_columns(given, other_column, width)
    for b in range(2):
        arrived = jnp.stack([lowers[first][b] + lowers[second][b] for first, second in zip(own, theirs)])
        gradient = gradient + place_columns(arrived, before[b, 1], width)
    return gradient


def solution(mesh):
    return jax.shard_map(
        body,
        mesh=mesh,
        in_specs=(
            P(),
            P("depth", None, ("groups", "scan"), None),
            P(("groups", "scan"), None),
            P(("groups", "scan")),
            P(("groups", "scan"), None, None),
        ),
        out_specs=P("depth", None, ("groups", "scan"), None),
        check_vma=False,
    )
```
